512 devices in a mesh: patch: 16 (over y, x_hi, core), map: 32 (over x_lo, z).
Axes of the slice: x: 4 (x_hi: 2, x_lo: 2; x = x_hi * 2 + x_lo), y: 4, z: 16, core: 2. Of those that a mesh axis runs over, the one named last changes fastest.
Arguments:
- maps: bfloat16 [64, 32, 24576], P('map', None, 'patch'), may hold values from -6 to 6
- cotangent: bfloat16 [64, 32, 24576], P('map', None, 'patch'), may hold values from -6 to 6
- tiles: bfloat16 [96, 3, 256, 256], P('patch'), may hold values from -0.21875 to 0.21875
- columns: int32 [96, 3], P('patch'), may hold values from 0 to 95, as said below
- filters: bfloat16 [3, 32, 32], replicated, may hold values from -0.625 to 0.625
Outputs:
- output: bfloat16 [64, 32, 24576], P('map', None, 'patch')
- input_grad: bfloat16 [64, 32, 24576], P('map', None, 'patch')
- filter_grad: float32 [3, 32, 32], replicated
The draws below stay inside these ranges and needn't reach their ends.
Inputs may be any that keep to these rules, and one draw needn't show every extreme that they name: `columns`: slot 0 of block row b names block b itself, slot 1 a block 1 to 2 before it and slot 2 a block 1 to 2 after it, counted cyclically over the 96 blocks; block row 0 reads exactly 2 blocks away on both sides.
All inputs are finite; a program needn't handle non-finite values.
Results may differ from the reference program's by a relative error of at most 0.0054.
Values may be sent and summed in bfloat16 or wider, within the bound.
No kernel may reach another device: no remote copies, remote signals or barrier semaphores. Data moves between devices by JAX's collectives and lax.ppermute only.
A program may use at most 64 MiB of HBM per device.

```python
import math
import jax
import jax.numpy as jnp
from jax import lax

C = 32
ORDER = 3
BS = 256
SLOTS = 3
REACH = 2
MAP_DEV = 2
NBLK = 96
NPIX = 24576
MAPS = 64
N_MAP = 32


def draw_columns(key, part):
    left_key = jax.random.fold_in(key, 11)
    right_key = jax.random.fold_in(key, 23)
    block_ids = jnp.arange(NBLK, dtype=jnp.int32)
    back_step = jax.random.randint(left_key, (NBLK,), 1, REACH + 1, dtype=jnp.int32)
    next_step = jax.random.randint(right_key, (NBLK,), 1, REACH + 1, dtype=jnp.int32)
    back_step = back_step.at[0].set(REACH)
    next_step = next_step.at[0].set(REACH)
    return jnp.stack([block_ids, (block_ids - back_step) % NBLK, (block_ids + next_step) % NBLK], axis=1)


def block_scale(rng, dims, split, least, high):
    def one(dim, blocks):
        heights = jax.random.uniform(jax.random.fold_in(jax.random.fold_in(rng, 6), dim), (blocks,), jnp.float32, least / len(split), high / len(split))
        return jnp.repeat(jnp.exp(heights), dims[dim] // blocks).reshape((-1,) + (1,) * (len(dims) - dim - 1))

    level = one(*split[0])
    for cut in split[1:]:
        level = level * one(*cut)
    return level


def bell_draw(key, extent, scale, reach, cuts=(), held_as=jnp.bfloat16):
    values = scale * jax.random.normal(key, extent, jnp.float32)
    if cuts:
        values = values * block_scale(key, extent, cuts, -0.22, 0.18)
    return jnp.clip(values, -reach, reach).astype(held_as)


def setup_inputs(seed: int = 0) -> dict:
    seeds = jax.random.split(jax.random.key(seed), 6)
    maps = bell_draw(seeds[0], (MAPS, C, NPIX), 1.0, 6.0, ((0, 32), (2, 16)))
    cotangent = bell_draw(seeds[1], (MAPS, C, NPIX), 1.0, 6.0, ((0, 32), (2, 16)))
    tiles = bell_draw(seeds[2], (NBLK, SLOTS, BS, BS), (SLOTS * BS) ** -0.5, 0.21875, ((0, 16),))
    columns = draw_columns(jax.random.fold_in(seeds[5], 71), 0)
    filters = bell_draw(seeds[4], (ORDER, C, C), (ORDER * C) ** -0.5, 0.625)
    return dict(maps=maps, cotangent=cotangent, tiles=tiles, columns=columns, filters=filters)


def forward_apply(field, tiles_f, columns, block_count, block_size):
    ext_blocks = field.reshape(field.shape[0], block_count, block_size)
    picked = ext_blocks[:, columns]
    result = jnp.einsum('nbjq,bjiq->nbi', picked, tiles_f)
    return result.reshape(field.shape[0], block_count * block_size)

def adjoint_apply(field, tiles_f, columns, block_count, block_size):
    grad_blocks = field.reshape(field.shape[0], block_count, block_size)
    contrib = jnp.einsum('nbi,bjiq->nbjq', grad_blocks, tiles_f)
    summed = jnp.zeros_like(grad_blocks).at[:, columns].add(contrib)
    return summed.reshape(field.shape[0], block_count * block_size)

def reference(maps, cotangent, tiles, columns, filters):
    tiles_f = tiles.astype(jnp.float32)
    weights_f = filters.astype(jnp.float32)
    row_count = MAP_DEV * C

    def one_group(pair):
        map_group, cot_group = pair
        x_zero = map_group.astype(jnp.float32).reshape(row_count, NPIX)
        x_one = forward_apply(x_zero, tiles_f, columns, NBLK, BS).astype(jnp.bfloat16)
        x_two = (2.0 * forward_apply(x_one.astype(jnp.float32), tiles_f, columns, NBLK, BS) - x_zero).astype(jnp.bfloat16)
        terms = jnp.stack([map_group, x_one.reshape(MAP_DEV, C, NPIX), x_two.reshape(MAP_DEV, C, NPIX)]).astype(jnp.float32)
        output = jnp.einsum('kco,kmcp->mop', weights_f, terms).astype(jnp.bfloat16)
        cot_f = cot_group.astype(jnp.float32)
        grads = jnp.einsum('kco,mop->kmcp', weights_f, cot_f)
        grad_two = grads[2].astype(jnp.bfloat16).reshape(row_count, NPIX)
        adj_first = adjoint_apply(grad_two.astype(jnp.float32), tiles_f, columns, NBLK, BS)
        update = (grads[1].reshape(row_count, NPIX) + 2.0 * adj_first).astype(jnp.bfloat16)
        adj_second = adjoint_apply(update.astype(jnp.float32), tiles_f, columns, NBLK, BS)
        input_grad = (grads[0].reshape(row_count, NPIX) - grad_two.astype(jnp.float32) + adj_second).astype(jnp.bfloat16)
        partial_grad = jnp.einsum('kmcp,mop->kco', terms, cot_f)
        return (output, input_grad.reshape(MAP_DEV, C, NPIX), partial_grad)
    map_groups = maps.reshape(N_MAP, MAP_DEV, C, NPIX)
    cot_groups = cotangent.reshape(N_MAP, MAP_DEV, C, NPIX)
    outputs, input_grads, partials = lax.map(one_group, (map_groups, cot_groups))
    scale = 1.0 / math.sqrt(MAPS * NPIX)
    filter_grad = lax.optimization_barrier(jnp.sum(partials, axis=0)) * scale
    return (outputs.reshape(MAPS, C, NPIX), input_grads.reshape(MAPS, C, NPIX), filter_grad)
```

```python
import math

import jax
import jax.numpy as jnp
from jax import lax
from jax.sharding import PartitionSpec as P

REACH = 2


def butterfly_sum(x, axes):
    for axis in axes:
        count = lax.axis_size(axis)
        step = 1
        while step < count:
            x = x + lax.ppermute(x, axis, [(i, i ^ step) for i in range(count)])
            step *= 2
    return x


def per_device(maps, cotangent, tiles, columns, filters):
    map_count, chan_count, pix_count = maps.shape
    block_count = tiles.shape[0]
    block_size = tiles.shape[2]
    row_count = map_count * chan_count
    patch_count = lax.axis_size("patch")
    total_blocks = block_count * patch_count
    first_block = lax.axis_index("patch") * block_count
    row_ids = first_block + jnp.arange(block_count, dtype=jnp.int32)
    back_one = ((row_ids - columns[:, 1]) % total_blocks == 1)[None, :, None]
    next_one = ((columns[:, 2] - row_ids) % total_blocks == 1)[None, :, None]
    nb = block_count
    to_right = [(i, (i + 1) % patch_count) for i in range(patch_count)]
    to_left = [((i + 1) % patch_count, i) for i in range(patch_count)]

    def exchange(edge_left, edge_right):
        from_right = lax.ppermute(edge_left, "patch", to_left)
        from_left = lax.ppermute(edge_right, "patch", to_right)
        return from_left, from_right

    def forward_local(ext):
        s0 = ext[:, 2 : 2 + nb]
        s1 = jnp.where(back_one, ext[:, 1 : 1 + nb], ext[:, 0:nb])
        s2 = jnp.where(next_one, ext[:, 3 : 3 + nb], ext[:, 4 : 4 + nb])
        picked = jnp.stack([s0, s1, s2], axis=2).astype(jnp.bfloat16)
        return jnp.einsum("nrjq,rjiq->nri", picked, tiles, preferred_element_type=jnp.float32)

    def adjoint_window(grads):
        contrib = jnp.einsum("nri,rjiq->nrjq", grads, tiles, preferred_element_type=jnp.float32)
        c0, c1, c2 = contrib[:, :, 0], contrib[:, :, 1], contrib[:, :, 2]
        zero = jnp.zeros_like(c0)
        pad = lambda v, lo: jnp.pad(v, ((0, 0), (lo, 4 - lo), (0, 0)))
        return (
            pad(c0, 2)
            + pad(jnp.where(back_one, c1, zero), 1)
            + pad(jnp.where(back_one, zero, c1), 0)
            + pad(jnp.where(next_one, c2, zero), 3)
            + pad(jnp.where(next_one, zero, c2), 4)
        )

    x_zero = maps.reshape(row_count, nb, block_size)
    weights = filters
    grads = jnp.einsum("kco,mop->kmcp", weights, cotangent, preferred_element_type=jnp.float32)
    grads = grads.reshape(3, row_count, nb, block_size)
    grad_two = grads[2].astype(jnp.bfloat16)

    win1 = adjoint_window(grad_two)
    x0f = x_zero.astype(jnp.float32)
    send_left = jnp.stack([x0f[:, 0:2], win1[:, 0:2]])
    send_right = jnp.stack([x0f[:, nb - 2 : nb], win1[:, nb + 2 : nb + 4]])
    got_left, got_right = exchange(send_left, send_right)
    ext0 = jnp.concatenate([got_left[0], x0f, got_right[0]], axis=1)
    x_one = forward_local(ext0).astype(jnp.bfloat16)
    adj1 = win1[:, 2 : 2 + nb]
    adj1 = adj1.at[:, 0:2].add(got_left[1])
    adj1 = adj1.at[:, nb - 2 : nb].add(got_right[1])
    update = (grads[1] + 2.0 * adj1).astype(jnp.bfloat16)

    win2 = adjoint_window(update)
    x1f = x_one.astype(jnp.float32)
    send_left = jnp.stack([x1f[:, 0:2], win2[:, 0:2]])
    send_right = jnp.stack([x1f[:, nb - 2 : nb], win2[:, nb + 2 : nb + 4]])
    got_left, got_right = exchange(send_left, send_right)
    ext1 = jnp.concatenate([got_left[0], x1f, got_right[0]], axis=1)
    x_two = (2.0 * forward_local(ext1) - x0f).astype(jnp.bfloat16)
    adj2 = win2[:, 2 : 2 + nb]
    adj2 = adj2.at[:, 0:2].add(got_left[1])
    adj2 = adj2.at[:, nb - 2 : nb].add(got_right[1])
    input_grad = (grads[0] - grad_two.astype(jnp.float32) + adj2).astype(jnp.bfloat16)

    shape3 = (map_count, chan_count, pix_count)
    terms = jnp.stack([maps, x_one.reshape(shape3), x_two.reshape(shape3)])
    output = jnp.einsum("kco,kmcp->mop", filters, terms, preferred_element_type=jnp.float32).astype(
        jnp.bfloat16
    )
    scale = 1.0 / math.sqrt(map_count * lax.axis_size("map") * pix_count * patch_count)
    local_grad = jnp.einsum("kmcp,mop->kco", terms, cotangent, preferred_element_type=jnp.float32)
    filter_grad = butterfly_sum(local_grad, ("patch", "map")) * scale
    return (output, input_grad.reshape(shape3), filter_grad)


def solution(mesh):
    placed = (
        P("map", None, "patch"),
        P("map", None, "patch"),
        P("patch", None, None, None),
        P("patch", None),
        P(),
    )
    return jax.shard_map(
        per_device,
        mesh=mesh,
        in_specs=placed,
        out_specs=(P("map", None, "patch"), P("map", None, "patch"), P()),
        check_vma=False,
    )
```

```python
import math

import jax
import jax.numpy as jnp
from jax import lax
from jax.sharding import PartitionSpec as P

REACH = 2


def ring_partner(coord, size, level):
    if size == 4 and level == 1:
        return (coord + 1) % size if coord % 2 else (coord - 1) % size
    return coord ^ (1 << level)


def torus_steps(patch_count, map_count):
    def coords(p, m):
        return dict(y=p // 4, x=((p // 2) % 2) * 2 + m // 16, z=m % 16, core=p % 2)

    def linear(c):
        p = c["y"] * 4 + (c["x"] // 2) * 2 + c["core"]
        return p * map_count + (c["x"] % 2) * 16 + c["z"]

    sizes = dict(core=2, x=4, y=4, z=16)
    plan = [("core", 0), ("x", 0), ("x", 1), ("y", 0), ("y", 1), ("z", 0), ("z", 1)]
    steps = []
    for name, level in plan:
        pairs = []
        for p in range(patch_count):
            for m in range(map_count):
                c = coords(p, m)
                d = dict(c)
                d[name] = ring_partner(c[name], sizes[name], level)
                pairs.append((linear(c), linear(d)))
        steps.append(pairs)
    for odd_up in (False, True):
        pairs = []
        for p in range(patch_count):
            for m in range(map_count):
                c = coords(p, m)
                d = dict(c)
                g = c["z"] // 4
                if not odd_up:
                    d["z"] = c["z"] ^ 4
                else:
                    d["z"] = (c["z"] + 4) % 16 if g % 2 else (c["z"] - 4) % 16
                pairs.append((linear(c), linear(d)))
        steps.append(pairs)
    return steps


def butterfly_sum(x, axes):
    patch_count, map_count = (lax.axis_size(a) for a in axes)
    if (patch_count, map_count) == (16, 32):
        for pairs in torus_steps(patch_count, map_count):
            x = x + lax.ppermute(x, axes, pairs)
        return x
    for axis in axes:
        count = lax.axis_size(axis)
        step = 1
        while step < count:
            x = x + lax.ppermute(x, axis, [(i, i ^ step) for i in range(count)])
            step *= 2
    return x


def per_device(maps, cotangent, tiles, columns, filters):
    map_count, chan_count, pix_count = maps.shape
    block_count = tiles.shape[0]
    block_size = tiles.shape[2]
    row_count = map_count * chan_count
    patch_count = lax.axis_size("patch")
    total_blocks = block_count * patch_count
    first_block = lax.axis_index("patch") * block_count
    row_ids = first_block + jnp.arange(block_count, dtype=jnp.int32)
    back_one = ((row_ids - columns[:, 1]) % total_blocks == 1)[None, :, None]
    next_one = ((columns[:, 2] - row_ids) % total_blocks == 1)[None, :, None]
    nb = block_count
    to_right = [(i, (i + 1) % patch_count) for i in range(patch_count)]
    to_left = [((i + 1) % patch_count, i) for i in range(patch_count)]

    def exchange(edge_left, edge_right):
        from_right = lax.ppermute(edge_left, "patch", to_left)
        from_left = lax.ppermute(edge_right, "patch", to_right)
        return from_left, from_right

    def forward_local(ext):
        s0 = ext[:, 2 : 2 + nb]
        s1 = jnp.where(back_one, ext[:, 1 : 1 + nb], ext[:, 0:nb])
        s2 = jnp.where(next_one, ext[:, 3 : 3 + nb], ext[:, 4 : 4 + nb])
        picked = jnp.stack([s0, s1, s2], axis=2).astype(jnp.bfloat16)
        return jnp.einsum("nrjq,rjiq->nri", picked, tiles, preferred_element_type=jnp.float32)

    def adjoint_window(grads):
        contrib = jnp.einsum("nri,rjiq->nrjq", grads, tiles, preferred_element_type=jnp.float32)
        c0, c1, c2 = contrib[:, :, 0], contrib[:, :, 1], contrib[:, :, 2]
        zero = jnp.zeros_like(c0)
        pad = lambda v, lo: jnp.pad(v, ((0, 0), (lo, 4 - lo), (0, 0)))
        return (
            pad(c0, 2)
            + pad(jnp.where(back_one, c1, zero), 1)
            + pad(jnp.where(back_one, zero, c1), 0)
            + pad(jnp.where(next_one, c2, zero), 3)
            + pad(jnp.where(next_one, zero, c2), 4)
        )

    x_zero = maps.reshape(row_count, nb, block_size)
    weights = filters
    grads = jnp.einsum("kco,mop->kmcp", weights, cotangent, preferred_element_type=jnp.float32)
    grads = grads.reshape(3, row_count, nb, block_size)
    grad_two = grads[2].astype(jnp.bfloat16)

    win1 = adjoint_window(grad_two)
    x0f = x_zero.astype(jnp.float32)
    send_left = jnp.stack([x0f[:, 0:2], win1[:, 0:2]])
    send_right = jnp.stack([x0f[:, nb - 2 : nb], win1[:, nb + 2 : nb + 4]])
    got_left, got_right = exchange(send_left, send_right)
    ext0 = jnp.concatenate([got_left[0], x0f, got_right[0]], axis=1)
    x_one = forward_local(ext0).astype(jnp.bfloat16)
    adj1 = win1[:, 2 : 2 + nb]
    adj1 = adj1.at[:, 0:2].add(got_left[1])
    adj1 = adj1.at[:, nb - 2 : nb].add(got_right[1])
    update = (grads[1] + 2.0 * adj1).astype(jnp.bfloat16)

    win2 = adjoint_window(update)
    x1f = x_one.astype(jnp.float32)
    send_left = jnp.stack([x1f[:, 0:2], win2[:, 0:2]])
    send_right = jnp.stack([x1f[:, nb - 2 : nb], win2[:, nb + 2 : nb + 4]])
    got_left, got_right = exchange(send_left, send_right)
    ext1 = jnp.concatenate([got_left[0], x1f, got_right[0]], axis=1)
    x_two = (2.0 * forward_local(ext1) - x0f).astype(jnp.bfloat16)
    adj2 = win2[:, 2 : 2 + nb]
    adj2 = adj2.at[:, 0:2].add(got_left[1])
    adj2 = adj2.at[:, nb - 2 : nb].add(got_right[1])
    input_grad = (grads[0] - grad_two.astype(jnp.float32) + adj2).astype(jnp.bfloat16)

    shape3 = (map_count, chan_count, pix_count)
    terms = jnp.stack([maps, x_one.reshape(shape3), x_two.reshape(shape3)])
    output = jnp.einsum("kco,kmcp->mop", filters, terms, preferred_element_type=jnp.float32).astype(
        jnp.bfloat16
    )
    scale = 1.0 / math.sqrt(map_count * lax.axis_size("map") * pix_count * patch_count)
    local_grad = jnp.einsum("kmcp,mop->kco", terms, cotangent, preferred_element_type=jnp.float32)
    filter_grad = butterfly_sum(local_grad, ("patch", "map")) * scale
    return (output, input_grad.reshape(shape3), filter_grad)


def solution(mesh):
    placed = (
        P("map", None, "patch"),
        P("map", None, "patch"),
        P("patch", None, None, None),
        P("patch", None),
        P(),
    )
    return jax.shard_map(
        per_device,
        mesh=mesh,
        in_specs=placed,
        out_specs=(P("map", None, "patch"), P("map", None, "patch"), P()),
        check_vma=False,
    )
```

```python
import math

import jax
import jax.numpy as jnp
from jax import lax
from jax.sharding import PartitionSpec as P

REACH = 2


def ring_partner(coord, size, level):
    if size == 4 and level == 1:
        return (coord + 1) % size if coord % 2 else (coord - 1) % size
    return coord ^ (1 << level)


def torus_steps(patch_count, map_count):
    def coords(p, m):
        return dict(y=p // 4, x=((p // 2) % 2) * 2 + m // 16, z=m % 16, core=p % 2)

    def linear(c):
        p = c["y"] * 4 + (c["x"] // 2) * 2 + c["core"]
        return p * map_count + (c["x"] % 2) * 16 + c["z"]

    sizes = dict(core=2, x=4, y=4, z=16)
    plan = [("core", 0), ("x", 0), ("x", 1), ("y", 0), ("y", 1), ("z", 0), ("z", 1)]
    steps = []
    for name, level in plan:
        pairs = []
        for p in range(patch_count):
            for m in range(map_count):
                c = coords(p, m)
                d = dict(c)
                d[name] = ring_partner(c[name], sizes[name], level)
                pairs.append((linear(c), linear(d)))
        steps.append(pairs)
    for odd_up in (False, True):
        pairs = []
        for p in range(patch_count):
            for m in range(map_count):
                c = coords(p, m)
                d = dict(c)
                g = c["z"] // 4
                if not odd_up:
                    d["z"] = c["z"] ^ 4
                else:
                    d["z"] = (c["z"] + 4) % 16 if g % 2 else (c["z"] - 4) % 16
                pairs.append((linear(c), linear(d)))
        steps.append(pairs)
    return steps


def butterfly_sum(x, axes):
    patch_count, map_count = (lax.axis_size(a) for a in axes)
    if (patch_count, map_count) == (16, 32):
        for pairs in torus_steps(patch_count, map_count):
            x = x + lax.ppermute(x, axes, pairs)
        return x
    for axis in axes:
        count = lax.axis_size(axis)
        step = 1
        while step < count:
            x = x + lax.ppermute(x, axis, [(i, i ^ step) for i in range(count)])
            step *= 2
    return x


def per_device(maps, cotangent, tiles, columns, filters):
    map_count, chan_count, pix_count = maps.shape
    block_count = tiles.shape[0]
    block_size = tiles.shape[2]
    row_count = map_count * chan_count
    patch_count = lax.axis_size("patch")
    total_blocks = block_count * patch_count
    first_block = lax.axis_index("patch") * block_count
    row_ids = first_block + jnp.arange(block_count, dtype=jnp.int32)
    back_one = ((row_ids - columns[:, 1]) % total_blocks == 1)[None, :, None]
    next_one = ((columns[:, 2] - row_ids) % total_blocks == 1)[None, :, None]
    nb = block_count
    to_right = [(i, (i + 1) % patch_count) for i in range(patch_count)]
    to_left = [((i + 1) % patch_count, i) for i in range(patch_count)]

    def exchange(edge_left, edge_right):
        from_right = lax.ppermute(edge_left, "patch", to_left)
        from_left = lax.ppermute(edge_right, "patch", to_right)
        return from_left, from_right

    def forward_local(ext):
        s0 = ext[:, 2 : 2 + nb]
        s1 = jnp.where(back_one, ext[:, 1 : 1 + nb], ext[:, 0:nb])
        s2 = jnp.where(next_one, ext[:, 3 : 3 + nb], ext[:, 4 : 4 + nb])
        picked = jnp.stack([s0, s1, s2], axis=2).astype(jnp.bfloat16)
        return jnp.einsum("nrjq,rjiq->nri", picked, tiles, preferred_element_type=jnp.float32)

    def adjoint_window(grads):
        contrib = jnp.einsum("nri,rjiq->nrjq", grads, tiles, preferred_element_type=jnp.float32)
        c0, c1, c2 = contrib[:, :, 0], contrib[:, :, 1], contrib[:, :, 2]
        zero = jnp.zeros_like(c0)
        pad = lambda v, lo: jnp.pad(v, ((0, 0), (lo, 4 - lo), (0, 0)))
        return (
            pad(c0, 2)
            + pad(jnp.where(back_one, c1, zero), 1)
            + pad(jnp.where(back_one, zero, c1), 0)
            + pad(jnp.where(next_one, c2, zero), 3)
            + pad(jnp.where(next_one, zero, c2), 4)
        )

    x_zero = maps.reshape(row_count, nb, block_size)
    weights = filters
    grads = jnp.einsum("kco,mop->kmcp", weights, cotangent, preferred_element_type=jnp.float32)
    grads = grads.reshape(3, row_count, nb, block_size)
    grad_two = grads[2].astype(jnp.bfloat16)

    win1 = adjoint_window(grad_two)
    cot_rows = cotangent.reshape(row_count, nb, block_size)
    winc = adjoint_window(cot_rows)
    x0f = x_zero.astype(jnp.float32)
    send_left = jnp.stack([x0f[:, 0:2], win1[:, 0:2], winc[:, 0:2]])
    send_right = jnp.stack(
        [x0f[:, nb - 2 : nb], win1[:, nb + 2 : nb + 4], winc[:, nb + 2 : nb + 4]]
    )
    got_left, got_right = exchange(send_left, send_right)
    ext0 = jnp.concatenate([got_left[0], x0f, got_right[0]], axis=1)
    x_one = forward_local(ext0).astype(jnp.bfloat16)
    adj1 = win1[:, 2 : 2 + nb]
    adj1 = adj1.at[:, 0:2].add(got_left[1])
    adj1 = adj1.at[:, nb - 2 : nb].add(got_right[1])
    update = (grads[1] + 2.0 * adj1).astype(jnp.bfloat16)
    lt_cot = winc[:, 2 : 2 + nb]
    lt_cot = lt_cot.at[:, 0:2].add(got_left[2])
    lt_cot = lt_cot.at[:, nb - 2 : nb].add(got_right[2])

    shape3 = (map_count, chan_count, pix_count)
    x_one3 = x_one.reshape(shape3)
    g_zero = jnp.einsum("mcp,mop->co", maps, cotangent, preferred_element_type=jnp.float32)
    g_one = jnp.einsum("mcp,mop->co", x_one3, cotangent, preferred_element_type=jnp.float32)
    g_cross = jnp.einsum(
        "mcp,mop->co",
        x_one3.astype(jnp.float32),
        lt_cot.reshape(shape3),
        preferred_element_type=jnp.float32,
        precision=lax.Precision.HIGHEST,
    )
    local_grad = jnp.stack([g_zero, g_one, 2.0 * g_cross - g_zero])
    scale = 1.0 / math.sqrt(map_count * lax.axis_size("map") * pix_count * patch_count)
    filter_grad = butterfly_sum(local_grad, ("patch", "map")) * scale

    win2 = adjoint_window(update)
    x1f = x_one.astype(jnp.float32)
    send_left = jnp.stack([x1f[:, 0:2], win2[:, 0:2]])
    send_right = jnp.stack([x1f[:, nb - 2 : nb], win2[:, nb + 2 : nb + 4]])
    got_left, got_right = exchange(send_left, send_right)
    ext1 = jnp.concatenate([got_left[0], x1f, got_right[0]], axis=1)
    x_two = (2.0 * forward_local(ext1) - x0f).astype(jnp.bfloat16)
    adj2 = win2[:, 2 : 2 + nb]
    adj2 = adj2.at[:, 0:2].add(got_left[1])
    adj2 = adj2.at[:, nb - 2 : nb].add(got_right[1])
    input_grad = (grads[0] - grad_two.astype(jnp.float32) + adj2).astype(jnp.bfloat16)

    terms = jnp.stack([maps, x_one3, x_two.reshape(shape3)])
    output = jnp.einsum("kco,kmcp->mop", filters, terms, preferred_element_type=jnp.float32).astype(
        jnp.bfloat16
    )
    return (output, input_grad.reshape(shape3), filter_grad)


def solution(mesh):
    placed = (
        P("map", None, "patch"),
        P("map", None, "patch"),
        P("patch", None, None, None),
        P("patch", None),
        P(),
    )
    return jax.shard_map(
        per_device,
        mesh=mesh,
        in_specs=placed,
        out_specs=(P("map", None, "patch"), P("map", None, "patch"), P()),
        check_vma=False,
    )
```

```python
import math

import jax
import jax.numpy as jnp
from jax import lax
from jax.sharding import PartitionSpec as P

REACH = 2


def ring_partner(coord, size, level):
    if size == 4 and level == 1:
        return (coord + 1) % size if coord % 2 else (coord - 1) % size
    return coord ^ (1 << level)


def torus_steps(patch_count, map_count):
    def coords(p, m):
        return dict(y=p // 4, x=((p // 2) % 2) * 2 + m // 16, z=m % 16, core=p % 2)

    def linear(c):
        p = c["y"] * 4 + (c["x"] // 2) * 2 + c["core"]
        return p * map_count + (c["x"] % 2) * 16 + c["z"]

    sizes = dict(core=2, x=4, y=4, z=16)
    plan = [("core", 0), ("x", 0), ("x", 1), ("y", 0), ("y", 1), ("z", 0), ("z", 1)]
    steps = []
    for name, level in plan:
        pairs = []
        for p in range(patch_count):
            for m in range(map_count):
                c = coords(p, m)
                d = dict(c)
                d[name] = ring_partner(c[name], sizes[name], level)
                pairs.append((linear(c), linear(d)))
        steps.append(pairs)
    for odd_up in (False, True):
        pairs = []
        for p in range(patch_count):
            for m in range(map_count):
                c = coords(p, m)
                d = dict(c)
                g = c["z"] // 4
                if not odd_up:
                    d["z"] = c["z"] ^ 4
                else:
                    d["z"] = (c["z"] + 4) % 16 if g % 2 else (c["z"] - 4) % 16
                pairs.append((linear(c), linear(d)))
        steps.append(pairs)
    return steps


def butterfly_sum(x, axes):
    patch_count, map_count = (lax.axis_size(a) for a in axes)
    if (patch_count, map_count) == (16, 32):
        for pairs in torus_steps(patch_count, map_count):
            x = x + lax.ppermute(x, axes, pairs)
        return x
    for axis in axes:
        count = lax.axis_size(axis)
        step = 1
        while step < count:
            x = x + lax.ppermute(x, axis, [(i, i ^ step) for i in range(count)])
            step *= 2
    return x


def per_device(maps, cotangent, tiles, columns, filters):
    map_count, chan_count, pix_count = maps.shape
    block_count = tiles.shape[0]
    block_size = tiles.shape[2]
    row_count = map_count * chan_count
    patch_count = lax.axis_size("patch")
    total_blocks = block_count * patch_count
    first_block = lax.axis_index("patch") * block_count
    row_ids = first_block + jnp.arange(block_count, dtype=jnp.int32)
    back_one = ((row_ids - columns[:, 1]) % total_blocks == 1)[:, None, None]
    next_one = ((columns[:, 2] - row_ids) % total_blocks == 1)[:, None, None]
    nb = block_count
    to_right = [(i, (i + 1) % patch_count) for i in range(patch_count)]
    to_left = [((i + 1) % patch_count, i) for i in range(patch_count)]

    def exchange(edge_left, edge_right):
        from_right = lax.ppermute(edge_left, "patch", to_left)
        from_left = lax.ppermute(edge_right, "patch", to_right)
        return from_left, from_right

    def to_blocks(field):
        return field.reshape(row_count, nb, block_size).transpose(1, 0, 2)

    def from_blocks(field):
        return field.transpose(1, 0, 2).reshape(map_count, chan_count, pix_count)

    def forward_local(ext):
        s0 = ext[2 : 2 + nb]
        s1 = jnp.where(back_one, ext[1 : 1 + nb], ext[0:nb])
        s2 = jnp.where(next_one, ext[3 : 3 + nb], ext[4 : 4 + nb])
        picked = jnp.stack([s0, s1, s2], axis=1).astype(jnp.bfloat16)
        return jnp.einsum("rjnq,rjiq->rni", picked, tiles, preferred_element_type=jnp.float32)

    def adjoint_window(grads):
        contrib = jnp.einsum("rni,rjiq->rjnq", grads, tiles, preferred_element_type=jnp.float32)
        c0, c1, c2 = contrib[:, 0], contrib[:, 1], contrib[:, 2]
        zero = jnp.zeros_like(c0)
        pad = lambda v, lo: jnp.pad(v, ((lo, 4 - lo), (0, 0), (0, 0)))
        return (
            pad(c0, 2)
            + pad(jnp.where(back_one, c1, zero), 1)
            + pad(jnp.where(back_one, zero, c1), 0)
            + pad(jnp.where(next_one, c2, zero), 3)
            + pad(jnp.where(next_one, zero, c2), 4)
        )

    x_zero = to_blocks(maps)
    cot_b = to_blocks(cotangent).reshape(nb, map_count, chan_count, block_size)
    grads = jnp.einsum("kco,rmop->krmcp", filters, cot_b, preferred_element_type=jnp.float32)
    grads = grads.reshape(3, nb, row_count, block_size)
    grad_two = grads[2].astype(jnp.bfloat16)

    win1 = adjoint_window(grad_two)
    x0f = x_zero.astype(jnp.float32)
    send_left = jnp.stack([x0f[0:2], win1[0:2]])
    send_right = jnp.stack([x0f[nb - 2 : nb], win1[nb + 2 : nb + 4]])
    got_left, got_right = exchange(send_left, send_right)
    ext0 = jnp.concatenate([got_left[0], x0f, got_right[0]], axis=0)
    x_one = forward_local(ext0).astype(jnp.bfloat16)
    adj1 = win1[2 : 2 + nb]
    adj1 = adj1.at[0:2].add(got_left[1])
    adj1 = adj1.at[nb - 2 : nb].add(got_right[1])
    update = (grads[1] + 2.0 * adj1).astype(jnp.bfloat16)

    win2 = adjoint_window(update)
    x1f = x_one.astype(jnp.float32)
    send_left = jnp.stack([x1f[0:2], win2[0:2]])
    send_right = jnp.stack([x1f[nb - 2 : nb], win2[nb + 2 : nb + 4]])
    got_left, got_right = exchange(send_left, send_right)
    ext1 = jnp.concatenate([got_left[0], x1f, got_right[0]], axis=0)
    x_two = (2.0 * forward_local(ext1) - x0f).astype(jnp.bfloat16)
    adj2 = win2[2 : 2 + nb]
    adj2 = adj2.at[0:2].add(got_left[1])
    adj2 = adj2.at[nb - 2 : nb].add(got_right[1])
    input_grad = (grads[0] - grad_two.astype(jnp.float32) + adj2).astype(jnp.bfloat16)

    split = (nb, map_count, chan_count, block_size)
    terms = jnp.stack([x_zero.reshape(split), x_one.reshape(split), x_two.reshape(split)])
    out_b = jnp.einsum("kco,krmcp->rmop", filters, terms, preferred_element_type=jnp.float32)
    output = from_blocks(out_b.astype(jnp.bfloat16).reshape(nb, row_count, block_size))
    scale = 1.0 / math.sqrt(map_count * lax.axis_size("map") * pix_count * patch_count)
    local_grad = jnp.einsum("krmcp,rmop->kco", terms, cot_b, preferred_element_type=jnp.float32)
    filter_grad = butterfly_sum(local_grad, ("patch", "map")) * scale
    return (output, from_blocks(input_grad), filter_grad)


def solution(mesh):
    placed = (
        P("map", None, "patch"),
        P("map", None, "patch"),
        P("patch", None, None, None),
        P("patch", None),
        P(),
    )
    return jax.shard_map(
        per_device,
        mesh=mesh,
        in_specs=placed,
        out_specs=(P("map", None, "patch"), P("map", None, "patch"), P()),
        check_vma=False,
    )
```

```python
import math

import jax
import jax.numpy as jnp
from jax import lax
from jax.sharding import PartitionSpec as P

REACH = 2


def ring_partner(coord, size, level):
    if size == 4 and level == 1:
        return (coord + 1) % size if coord % 2 else (coord - 1) % size
    return coord ^ (1 << level)


def torus_steps(patch_count, map_count):
    def coords(p, m):
        return dict(y=p // 4, x=((p // 2) % 2) * 2 + m // 16, z=m % 16, core=p % 2)

    def linear(c):
        p = c["y"] * 4 + (c["x"] // 2) * 2 + c["core"]
        return p * map_count + (c["x"] % 2) * 16 + c["z"]

    sizes = dict(core=2, x=4, y=4, z=16)
    plan = [("core", 0), ("x", 0), ("x", 1), ("y", 0), ("y", 1), ("z", 0), ("z", 1)]
    steps = []
    for name, level in plan:
        pairs = []
        for p in range(patch_count):
            for m in range(map_count):
                c = coords(p, m)
                d = dict(c)
                d[name] = ring_partner(c[name], sizes[name], level)
                pairs.append((linear(c), linear(d)))
        steps.append(pairs)
    for odd_up in (False, True):
        pairs = []
        for p in range(patch_count):
            for m in range(map_count):
                c = coords(p, m)
                d = dict(c)
                g = c["z"] // 4
                if not odd_up:
                    d["z"] = c["z"] ^ 4
                else:
                    d["z"] = (c["z"] + 4) % 16 if g % 2 else (c["z"] - 4) % 16
                pairs.append((linear(c), linear(d)))
        steps.append(pairs)
    return steps


def butterfly_sum(x, axes):
    patch_count, map_count = (lax.axis_size(a) for a in axes)
    if (patch_count, map_count) == (16, 32):
        for pairs in torus_steps(patch_count, map_count):
            x = x + lax.ppermute(x, axes, pairs)
        return x
    for axis in axes:
        count = lax.axis_size(axis)
        step = 1
        while step < count:
            x = x + lax.ppermute(x, axis, [(i, i ^ step) for i in range(count)])
            step *= 2
    return x


def per_device(maps, cotangent, tiles, columns, filters):
    map_count, chan_count, pix_count = maps.shape
    block_count = tiles.shape[0]
    block_size = tiles.shape[2]
    row_count = map_count * chan_count
    patch_count = lax.axis_size("patch")
    total_blocks = block_count * patch_count
    first_block = lax.axis_index("patch") * block_count
    row_ids = first_block + jnp.arange(block_count, dtype=jnp.int32)
    back_one = ((row_ids - columns[:, 1]) % total_blocks == 1)[:, None, None]
    next_one = ((columns[:, 2] - row_ids) % total_blocks == 1)[:, None, None]
    nb = block_count
    to_right = [(i, (i + 1) % patch_count) for i in range(patch_count)]
    to_left = [((i + 1) % patch_count, i) for i in range(patch_count)]

    def exchange(edge_left, edge_right):
        from_right = lax.ppermute(edge_left, "patch", to_left)
        from_left = lax.ppermute(edge_right, "patch", to_right)
        return from_left, from_right

    def to_blocks(field):
        return field.reshape(row_count, nb, block_size).transpose(1, 0, 2)

    def from_blocks(field):
        return field.transpose(1, 0, 2).reshape(map_count, chan_count, pix_count)

    def forward_local(ext):
        s0 = ext[2 : 2 + nb]
        s1 = jnp.where(back_one, ext[1 : 1 + nb], ext[0:nb])
        s2 = jnp.where(next_one, ext[3 : 3 + nb], ext[4 : 4 + nb])
        picked = jnp.stack([s0, s1, s2], axis=1).astype(jnp.bfloat16)
        return jnp.einsum("rjnq,rjiq->rni", picked, tiles, preferred_element_type=jnp.float32)

    def adjoint_window(grads):
        contrib = jnp.einsum("rni,rjiq->rjnq", grads, tiles, preferred_element_type=jnp.float32)
        c0, c1, c2 = contrib[:, 0], contrib[:, 1], contrib[:, 2]
        zero = jnp.zeros_like(c0)
        pad = lambda v, lo: jnp.pad(v, ((lo, 4 - lo), (0, 0), (0, 0)))
        return (
            pad(c0, 2)
            + pad(jnp.where(back_one, c1, zero), 1)
            + pad(jnp.where(back_one, zero, c1), 0)
            + pad(jnp.where(next_one, c2, zero), 3)
            + pad(jnp.where(next_one, zero, c2), 4)
        )

    x_zero = to_blocks(maps)
    cot_b = to_blocks(cotangent).reshape(nb, map_count, chan_count, block_size)
    grads = jnp.einsum("kco,rmop->krmcp", filters, cot_b, preferred_element_type=jnp.float32)
    grads = grads.reshape(3, nb, row_count, block_size)
    grad_two = grads[2].astype(jnp.bfloat16)

    win1 = adjoint_window(grad_two)
    x0f = x_zero.astype(jnp.float32)
    send_left = jnp.stack([x0f[0:2], win1[0:2]])
    send_right = jnp.stack([x0f[nb - 2 : nb], win1[nb + 2 : nb + 4]])
    got_left, got_right = exchange(send_left, send_right)
    ext0 = jnp.concatenate([got_left[0], x0f, got_right[0]], axis=0)
    x_one = forward_local(ext0).astype(jnp.bfloat16)
    adj1 = win1[2 : 2 + nb]
    adj1 = adj1.at[0:2].add(got_left[1])
    adj1 = adj1.at[nb - 2 : nb].add(got_right[1])
    update = (grads[1] + 2.0 * adj1).astype(jnp.bfloat16)

    win2 = adjoint_window(update)
    x1f = x_one.astype(jnp.float32)
    send_left = jnp.stack([x1f[0:2], win2[0:2]])
    send_right = jnp.stack([x1f[nb - 2 : nb], win2[nb + 2 : nb + 4]])
    got_left, got_right = exchange(send_left, send_right)
    ext1 = jnp.concatenate([got_left[0], x1f, got_right[0]], axis=0)
    x_two = (2.0 * forward_local(ext1) - x0f).astype(jnp.bfloat16)
    adj2 = win2[2 : 2 + nb]
    adj2 = adj2.at[0:2].add(got_left[1])
    adj2 = adj2.at[nb - 2 : nb].add(got_right[1])
    input_grad = (grads[0] - grad_two.astype(jnp.float32) + adj2).astype(jnp.bfloat16)

    split = (nb, map_count, chan_count, block_size)
    terms = jnp.stack([x_zero.reshape(split), x_one.reshape(split), x_two.reshape(split)])
    out_b = jnp.einsum("kco,krmcp->rmop", filters, terms, preferred_element_type=jnp.float32)
    output = from_blocks(out_b.astype(jnp.bfloat16).reshape(nb, row_count, block_size))
    scale = 1.0 / math.sqrt(map_count * lax.axis_size("map") * pix_count * patch_count)
    local_grad = jnp.einsum("krmcp,rmop->kco", terms, cot_b, preferred_element_type=jnp.float32)
    flat = local_grad.reshape(-1, 128)
    filter_grad = butterfly_sum(flat, ("patch", "map")).reshape(local_grad.shape) * scale
    return (output, from_blocks(input_grad), filter_grad)


def solution(mesh):
    placed = (
        P("map", None, "patch"),
        P("map", None, "patch"),
        P("patch", None, None, None),
        P("patch", None),
        P(),
    )
    return jax.shard_map(
        per_device,
        mesh=mesh,
        in_specs=placed,
        out_specs=(P("map", None, "patch"), P("map", None, "patch"), P()),
        check_vma=False,
    )
```

```python
import math

import jax
import jax.numpy as jnp
from jax import lax
from jax.sharding import PartitionSpec as P

REACH = 2


def ring_partner(coord, size, level):
    if size == 4 and level == 1:
        return (coord + 1) % size if coord % 2 else (coord - 1) % size
    return coord ^ (1 << level)


def torus_steps(patch_count, map_count):
    def coords(p, m):
        return dict(y=p // 4, x=((p // 2) % 2) * 2 + m // 16, z=m % 16, core=p % 2)

    def linear(c):
        p = c["y"] * 4 + (c["x"] // 2) * 2 + c["core"]
        return p * map_count + (c["x"] % 2) * 16 + c["z"]

    sizes = dict(core=2, x=4, y=4, z=16)
    plan = [("core", 0), ("x", 0), ("x", 1), ("y", 0), ("y", 1), ("z", 0), ("z", 1)]
    steps = []
    for name, level in plan:
        pairs = []
        for p in range(patch_count):
            for m in range(map_count):
                c = coords(p, m)
                d = dict(c)
                d[name] = ring_partner(c[name], sizes[name], level)
                pairs.append((linear(c), linear(d)))
        steps.append(pairs)
    for odd_up in (False, True):
        pairs = []
        for p in range(patch_count):
            for m in range(map_count):
                c = coords(p, m)
                d = dict(c)
                g = c["z"] // 4
                if not odd_up:
                    d["z"] = c["z"] ^ 4
                else:
                    d["z"] = (c["z"] + 4) % 16 if g % 2 else (c["z"] - 4) % 16
                pairs.append((linear(c), linear(d)))
        steps.append(pairs)
    return steps


def butterfly_sum(x, axes):
    patch_count, map_count = (lax.axis_size(a) for a in axes)
    if (patch_count, map_count) == (16, 32):
        for pairs in torus_steps(patch_count, map_count):
            x = x + lax.ppermute(x, axes, pairs)
        return x
    for axis in axes:
        count = lax.axis_size(axis)
        step = 1
        while step < count:
            x = x + lax.ppermute(x, axis, [(i, i ^ step) for i in range(count)])
            step *= 2
    return x


def per_device(maps, cotangent, tiles, columns, filters):
    map_count, chan_count, pix_count = maps.shape
    block_count = tiles.shape[0]
    block_size = tiles.shape[2]
    row_count = map_count * chan_count
    patch_count = lax.axis_size("patch")
    total_blocks = block_count * patch_count
    first_block = lax.axis_index("patch") * block_count
    row_ids = first_block + jnp.arange(block_count, dtype=jnp.int32)
    back_one = ((row_ids - columns[:, 1]) % total_blocks == 1)[:, None, None]
    next_one = ((columns[:, 2] - row_ids) % total_blocks == 1)[:, None, None]
    nb = block_count
    to_right = [(i, (i + 1) % patch_count) for i in range(patch_count)]
    to_left = [((i + 1) % patch_count, i) for i in range(patch_count)]

    def exchange(edge_left, edge_right):
        edge_left, edge_right = lax.optimization_barrier((edge_left, edge_right))
        from_right = lax.ppermute(edge_left, "patch", to_left)
        from_left = lax.ppermute(edge_right, "patch", to_right)
        return from_left, from_right

    def to_blocks(field):
        return field.reshape(row_count, nb, block_size).transpose(1, 0, 2)

    def from_blocks(field):
        return field.transpose(1, 0, 2).reshape(map_count, chan_count, pix_count)

    def forward_local(ext):
        s0 = ext[2 : 2 + nb]
        s1 = jnp.where(back_one, ext[1 : 1 + nb], ext[0:nb])
        s2 = jnp.where(next_one, ext[3 : 3 + nb], ext[4 : 4 + nb])
        picked = jnp.stack([s0, s1, s2], axis=1).astype(jnp.bfloat16)
        return jnp.einsum("rjnq,rjiq->rni", picked, tiles, preferred_element_type=jnp.float32)

    def adjoint_window(grads):
        contrib = jnp.einsum("rni,rjiq->rjnq", grads, tiles, preferred_element_type=jnp.float32)
        c0, c1, c2 = contrib[:, 0], contrib[:, 1], contrib[:, 2]
        zero = jnp.zeros_like(c0)
        pad = lambda v, lo: jnp.pad(v, ((lo, 4 - lo), (0, 0), (0, 0)))
        return (
            pad(c0, 2)
            + pad(jnp.where(back_one, c1, zero), 1)
            + pad(jnp.where(back_one, zero, c1), 0)
            + pad(jnp.where(next_one, c2, zero), 3)
            + pad(jnp.where(next_one, zero, c2), 4)
        )

    x_zero = to_blocks(maps)
    cot_b = to_blocks(cotangent).reshape(nb, map_count, chan_count, block_size)
    grads = jnp.einsum("kco,rmop->krmcp", filters, cot_b, preferred_element_type=jnp.float32)
    grads = grads.reshape(3, nb, row_count, block_size)
    grad_two = grads[2].astype(jnp.bfloat16)

    win1 = adjoint_window(grad_two)
    x0f = x_zero.astype(jnp.float32)
    send_left = jnp.stack([x0f[0:2], win1[0:2]])
    send_right = jnp.stack([x0f[nb - 2 : nb], win1[nb + 2 : nb + 4]])
    got_left, got_right = exchange(send_left, send_right)
    ext0 = jnp.concatenate([got_left[0], x0f, got_right[0]], axis=0)
    x_one = forward_local(ext0).astype(jnp.bfloat16)
    adj1 = win1[2 : 2 + nb]
    adj1 = adj1.at[0:2].add(got_left[1])
    adj1 = adj1.at[nb - 2 : nb].add(got_right[1])
    update = (grads[1] + 2.0 * adj1).astype(jnp.bfloat16)

    win2 = adjoint_window(update)
    x1f = x_one.astype(jnp.float32)
    send_left = jnp.stack([x1f[0:2], win2[0:2]])
    send_right = jnp.stack([x1f[nb - 2 : nb], win2[nb + 2 : nb + 4]])
    got_left, got_right = exchange(send_left, send_right)
    ext1 = jnp.concatenate([got_left[0], x1f, got_right[0]], axis=0)
    x_two = (2.0 * forward_local(ext1) - x0f).astype(jnp.bfloat16)
    adj2 = win2[2 : 2 + nb]
    adj2 = adj2.at[0:2].add(got_left[1])
    adj2 = adj2.at[nb - 2 : nb].add(got_right[1])
    input_grad = (grads[0] - grad_two.astype(jnp.float32) + adj2).astype(jnp.bfloat16)

    split = (nb, map_count, chan_count, block_size)
    terms = jnp.stack([x_zero.reshape(split), x_one.reshape(split), x_two.reshape(split)])
    out_b = jnp.einsum("kco,krmcp->rmop", filters, terms, preferred_element_type=jnp.float32)
    output = from_blocks(out_b.astype(jnp.bfloat16).reshape(nb, row_count, block_size))
    scale = 1.0 / math.sqrt(map_count * lax.axis_size("map") * pix_count * patch_count)
    local_grad = jnp.einsum("krmcp,rmop->kco", terms, cot_b, preferred_element_type=jnp.float32)
    flat = local_grad.reshape(-1, 128)
    filter_grad = butterfly_sum(flat, ("patch", "map")).reshape(local_grad.shape) * scale
    return (output, from_blocks(input_grad), filter_grad)


def solution(mesh):
    placed = (
        P("map", None, "patch"),
        P("map", None, "patch"),
        P("patch", None, None, None),
        P("patch", None),
        P(),
    )
    return jax.shard_map(
        per_device,
        mesh=mesh,
        in_specs=placed,
        out_specs=(P("map", None, "patch"), P("map", None, "patch"), P()),
        check_vma=False,
    )
```

```python
import math

import jax
import jax.numpy as jnp
from jax import lax
from jax.sharding import PartitionSpec as P

REACH = 2


def ring_partner(coord, size, level):
    if size == 4 and level == 1:
        return (coord + 1) % size if coord % 2 else (coord - 1) % size
    return coord ^ (1 << level)


def torus_steps(patch_count, map_count):
    def coords(p, m):
        return dict(y=p // 4, x=((p // 2) % 2) * 2 + m // 16, z=m % 16, core=p % 2)

    def linear(c):
        p = c["y"] * 4 + (c["x"] // 2) * 2 + c["core"]
        return p * map_count + (c["x"] % 2) * 16 + c["z"]

    sizes = dict(core=2, x=4, y=4, z=16)
    plan = [("core", 0), ("x", 0), ("x", 1), ("y", 0), ("y", 1), ("z", 0), ("z", 1)]
    steps = []
    for name, level in plan:
        pairs = []
        for p in range(patch_count):
            for m in range(map_count):
                c = coords(p, m)
                d = dict(c)
                d[name] = ring_partner(c[name], sizes[name], level)
                pairs.append((linear(c), linear(d)))
        steps.append(pairs)
    for odd_up in (False, True):
        pairs = []
        for p in range(patch_count):
            for m in range(map_count):
                c = coords(p, m)
                d = dict(c)
                g = c["z"] // 4
                if not odd_up:
                    d["z"] = c["z"] ^ 4
                else:
                    d["z"] = (c["z"] + 4) % 16 if g % 2 else (c["z"] - 4) % 16
                pairs.append((linear(c), linear(d)))
        steps.append(pairs)
    return steps


def butterfly_sum(x, axes):
    patch_count, map_count = (lax.axis_size(a) for a in axes)
    if (patch_count, map_count) == (16, 32):
        for pairs in torus_steps(patch_count, map_count):
            x = x + lax.ppermute(x, axes, pairs)
        return x
    for axis in axes:
        count = lax.axis_size(axis)
        step = 1
        while step < count:
            x = x + lax.ppermute(x, axis, [(i, i ^ step) for i in range(count)])
            step *= 2
    return x


def per_device(maps, cotangent, tiles, columns, filters):
    map_count, chan_count, pix_count = maps.shape
    block_count = tiles.shape[0]
    block_size = tiles.shape[2]
    row_count = map_count * chan_count
    patch_count = lax.axis_size("patch")
    total_blocks = block_count * patch_count
    first_block = lax.axis_index("patch") * block_count
    row_ids = first_block + jnp.arange(block_count, dtype=jnp.int32)
    back_one = ((row_ids - columns[:, 1]) % total_blocks == 1)[:, None, None]
    next_one = ((columns[:, 2] - row_ids) % total_blocks == 1)[:, None, None]
    nb = block_count
    to_right = [(i, (i + 1) % patch_count) for i in range(patch_count)]
    to_left = [((i + 1) % patch_count, i) for i in range(patch_count)]

    def exchange(edge_left, edge_right):
        edge_left, edge_right = lax.optimization_barrier((edge_left, edge_right))
        from_right = lax.ppermute(edge_left, "patch", to_left)
        from_left = lax.ppermute(edge_right, "patch", to_right)
        return from_left, from_right

    def to_blocks(field):
        return field.reshape(row_count, nb, block_size).transpose(1, 0, 2)

    def from_blocks(field):
        return field.transpose(1, 0, 2).reshape(map_count, chan_count, pix_count)

    def forward_local(ext):
        s0 = ext[2 : 2 + nb]
        s1 = jnp.where(back_one, ext[1 : 1 + nb], ext[0:nb])
        s2 = jnp.where(next_one, ext[3 : 3 + nb], ext[4 : 4 + nb])
        picked = jnp.stack([s0, s1, s2], axis=1).astype(jnp.bfloat16)
        return jnp.einsum("rjnq,rjiq->rni", picked, tiles, preferred_element_type=jnp.float32)

    def adjoint_window(grads):
        contrib = jnp.einsum("rni,rjiq->rjnq", grads, tiles, preferred_element_type=jnp.float32)
        c0, c1, c2 = contrib[:, 0], contrib[:, 1], contrib[:, 2]
        zero = jnp.zeros_like(c0)
        pad = lambda v, lo: jnp.pad(v, ((lo, 4 - lo), (0, 0), (0, 0)))
        return (
            pad(c0, 2)
            + pad(jnp.where(back_one, c1, zero), 1)
            + pad(jnp.where(back_one, zero, c1), 0)
            + pad(jnp.where(next_one, c2, zero), 3)
            + pad(jnp.where(next_one, zero, c2), 4)
        )

    x_zero = to_blocks(maps)
    cot_b = to_blocks(cotangent).reshape(nb, map_count, chan_count, block_size)
    grads = jnp.einsum("kco,rmop->krmcp", filters, cot_b, preferred_element_type=jnp.float32)
    grads = grads.reshape(3, nb, row_count, block_size)
    grad_two = grads[2].astype(jnp.bfloat16)

    by_block = cotangent.reshape(map_count, chan_count, nb, block_size)
    map_blocks = maps.reshape(row_count, nb, block_size)

    def edge_out(lo, slot):
        cot_edge = by_block[:, :, lo : lo + 2].transpose(2, 0, 1, 3)
        g_edge = jnp.einsum(
            "co,rmoq->rmcq", filters[2], cot_edge, preferred_element_type=jnp.float32
        ).astype(jnp.bfloat16).reshape(2, row_count, block_size)
        return jnp.einsum(
            "rni,riq->rnq", g_edge, tiles[lo : lo + 2, slot], preferred_element_type=jnp.float32
        )

    cl = edge_out(0, 1)
    cr = edge_out(nb - 2, 2)
    zero = jnp.zeros_like(cl[0])
    out_left = jnp.stack(
        [
            jnp.where(back_one[0], zero, cl[0]),
            jnp.where(back_one[0], cl[0], zero) + jnp.where(back_one[1], zero, cl[1]),
        ]
    )
    out_right = jnp.stack(
        [
            jnp.where(next_one[nb - 2], zero, cr[0]) + jnp.where(next_one[nb - 1], cr[1], zero),
            jnp.where(next_one[nb - 1], zero, cr[1]),
        ]
    )
    halo_left = map_blocks[:, 0:2].transpose(1, 0, 2).astype(jnp.float32)
    halo_right = map_blocks[:, nb - 2 : nb].transpose(1, 0, 2).astype(jnp.float32)
    send_left = jnp.stack([halo_left, out_left])
    send_right = jnp.stack([halo_right, out_right])
    win1 = adjoint_window(grad_two)
    x0f = x_zero.astype(jnp.float32)
    got_left, got_right = exchange(send_left, send_right)
    ext0 = jnp.concatenate([got_left[0], x0f, got_right[0]], axis=0)
    x_one = forward_local(ext0).astype(jnp.bfloat16)
    adj1 = win1[2 : 2 + nb]
    adj1 = adj1.at[0:2].add(got_left[1])
    adj1 = adj1.at[nb - 2 : nb].add(got_right[1])
    update = (grads[1] + 2.0 * adj1).astype(jnp.bfloat16)

    win2 = adjoint_window(update)
    x1f = x_one.astype(jnp.float32)
    send_left = jnp.stack([x1f[0:2], win2[0:2]])
    send_right = jnp.stack([x1f[nb - 2 : nb], win2[nb + 2 : nb + 4]])
    got_left, got_right = exchange(send_left, send_right)
    ext1 = jnp.concatenate([got_left[0], x1f, got_right[0]], axis=0)
    x_two = (2.0 * forward_local(ext1) - x0f).astype(jnp.bfloat16)
    adj2 = win2[2 : 2 + nb]
    adj2 = adj2.at[0:2].add(got_left[1])
    adj2 = adj2.at[nb - 2 : nb].add(got_right[1])
    input_grad = (grads[0] - grad_two.astype(jnp.float32) + adj2).astype(jnp.bfloat16)

    split = (nb, map_count, chan_count, block_size)
    terms = jnp.stack([x_zero.reshape(split), x_one.reshape(split), x_two.reshape(split)])
    out_b = jnp.einsum("kco,krmcp->rmop", filters, terms, preferred_element_type=jnp.float32)
    output = from_blocks(out_b.astype(jnp.bfloat16).reshape(nb, row_count, block_size))
    scale = 1.0 / math.sqrt(map_count * lax.axis_size("map") * pix_count * patch_count)
    local_grad = jnp.einsum("krmcp,rmop->kco", terms, cot_b, preferred_element_type=jnp.float32)
    filter_grad = butterfly_sum(local_grad, ("patch", "map")) * scale
    return (output, from_blocks(input_grad), filter_grad)


def solution(mesh):
    placed = (
        P("map", None, "patch"),
        P("map", None, "patch"),
        P("patch", None, None, None),
        P("patch", None),
        P(),
    )
    return jax.shard_map(
        per_device,
        mesh=mesh,
        in_specs=placed,
        out_specs=(P("map", None, "patch"), P("map", None, "patch"), P()),
        check_vma=False,
    )
```

```python
import math

import jax
import jax.numpy as jnp
from jax import lax
from jax.sharding import PartitionSpec as P

REACH = 2


def ring_partner(coord, size, level):
    if size == 4 and level == 1:
        return (coord + 1) % size if coord % 2 else (coord - 1) % size
    return coord ^ (1 << level)


def torus_steps(patch_count, map_count):
    def coords(p, m):
        return dict(y=p // 4, x=((p // 2) % 2) * 2 + m // 16, z=m % 16, core=p % 2)

    def linear(c):
        p = c["y"] * 4 + (c["x"] // 2) * 2 + c["core"]
        return p * map_count + (c["x"] % 2) * 16 + c["z"]

    sizes = dict(core=2, x=4, y=4, z=16)
    plan = [("core", 0), ("x", 0), ("x", 1), ("y", 0), ("y", 1), ("z", 0), ("z", 1)]
    steps = []
    for name, level in plan:
        pairs = []
        for p in range(patch_count):
            for m in range(map_count):
                c = coords(p, m)
                d = dict(c)
                d[name] = ring_partner(c[name], sizes[name], level)
                pairs.append((linear(c), linear(d)))
        steps.append(pairs)
    for odd_up in (False, True):
        pairs = []
        for p in range(patch_count):
            for m in range(map_count):
                c = coords(p, m)
                d = dict(c)
                g = c["z"] // 4
                if not odd_up:
                    d["z"] = c["z"] ^ 4
                else:
                    d["z"] = (c["z"] + 4) % 16 if g % 2 else (c["z"] - 4) % 16
                pairs.append((linear(c), linear(d)))
        steps.append(pairs)
    return steps


def butterfly_sum(x, axes):
    patch_count, map_count = (lax.axis_size(a) for a in axes)
    if (patch_count, map_count) == (16, 32):
        for pairs in torus_steps(patch_count, map_count):
            x = x + lax.ppermute(x, axes, pairs)
        return x
    for axis in axes:
        count = lax.axis_size(axis)
        step = 1
        while step < count:
            x = x + lax.ppermute(x, axis, [(i, i ^ step) for i in range(count)])
            step *= 2
    return x


def per_device(maps, cotangent, tiles, columns, filters):
    map_count, chan_count, pix_count = maps.shape
    block_count = tiles.shape[0]
    block_size = tiles.shape[2]
    row_count = map_count * chan_count
    patch_count = lax.axis_size("patch")
    total_blocks = block_count * patch_count
    first_block = lax.axis_index("patch") * block_count
    row_ids = first_block + jnp.arange(block_count, dtype=jnp.int32)
    back_one = ((row_ids - columns[:, 1]) % total_blocks == 1)[:, None, None]
    next_one = ((columns[:, 2] - row_ids) % total_blocks == 1)[:, None, None]
    nb = block_count
    to_right = [(i, (i + 1) % patch_count) for i in range(patch_count)]
    to_left = [((i + 1) % patch_count, i) for i in range(patch_count)]

    def exchange(edge_left, edge_right):
        edge_left, edge_right = lax.optimization_barrier((edge_left, edge_right))
        from_right = lax.ppermute(edge_left, "patch", to_left)
        from_left = lax.ppermute(edge_right, "patch", to_right)
        return from_left, from_right

    def to_blocks(field):
        return field.reshape(row_count, nb, block_size).transpose(1, 0, 2)

    def from_blocks(field):
        return field.transpose(1, 0, 2).reshape(map_count, chan_count, pix_count)

    def forward_local(ext):
        s0 = ext[2 : 2 + nb]
        s1 = jnp.where(back_one, ext[1 : 1 + nb], ext[0:nb])
        s2 = jnp.where(next_one, ext[3 : 3 + nb], ext[4 : 4 + nb])
        picked = jnp.stack([s0, s1, s2], axis=1).astype(jnp.bfloat16)
        return jnp.einsum("rjnq,rjiq->rni", picked, tiles, preferred_element_type=jnp.float32)

    def adjoint_window(grads):
        contrib = jnp.einsum("rni,rjiq->rjnq", grads, tiles, preferred_element_type=jnp.float32)
        c0, c1, c2 = contrib[:, 0], contrib[:, 1], contrib[:, 2]
        zero = jnp.zeros_like(c0)
        pad = lambda v, lo: jnp.pad(v, ((lo, 4 - lo), (0, 0), (0, 0)))
        return (
            pad(c0, 2)
            + pad(jnp.where(back_one, c1, zero), 1)
            + pad(jnp.where(back_one, zero, c1), 0)
            + pad(jnp.where(next_one, c2, zero), 3)
            + pad(jnp.where(next_one, zero, c2), 4)
        )

    x_zero = to_blocks(maps)
    cot_b = to_blocks(cotangent).reshape(nb, map_count, chan_count, block_size)
    grads = jnp.einsum("kco,rmop->krmcp", filters, cot_b, preferred_element_type=jnp.float32)
    grads = grads.reshape(3, nb, row_count, block_size)
    grad_two = grads[2].astype(jnp.bfloat16)

    win1 = adjoint_window(grad_two)
    x0f = x_zero.astype(jnp.float32)
    send_left = jnp.stack([x0f[0:2], win1[0:2]])
    send_right = jnp.stack([x0f[nb - 2 : nb], win1[nb + 2 : nb + 4]])
    got_left, got_right = exchange(send_left, send_right)
    ext0 = jnp.concatenate([got_left[0], x0f, got_right[0]], axis=0)
    x_one = forward_local(ext0).astype(jnp.bfloat16)
    adj1 = win1[2 : 2 + nb]
    adj1 = adj1.at[0:2].add(got_left[1])
    adj1 = adj1.at[nb - 2 : nb].add(got_right[1])
    update = (grads[1] + 2.0 * adj1).astype(jnp.bfloat16)

    win2 = adjoint_window(update)
    x1f = x_one.astype(jnp.float32)
    send_left = jnp.stack([x1f[0:2], win2[0:2]])
    send_right = jnp.stack([x1f[nb - 2 : nb], win2[nb + 2 : nb + 4]])
    got_left, got_right = exchange(send_left, send_right)
    ext1 = jnp.concatenate([got_left[0], x1f, got_right[0]], axis=0)
    x_two = (2.0 * forward_local(ext1) - x0f).astype(jnp.bfloat16)
    adj2 = win2[2 : 2 + nb]
    adj2 = adj2.at[0:2].add(got_left[1])
    adj2 = adj2.at[nb - 2 : nb].add(got_right[1])
    input_grad = (grads[0] - grad_two.astype(jnp.float32) + adj2).astype(jnp.bfloat16)

    split = (nb, map_count, chan_count, block_size)
    terms = jnp.stack([x_zero.reshape(split), x_one.reshape(split), x_two.reshape(split)])
    out_b = jnp.einsum("kco,krmcp->rmop", filters, terms, preferred_element_type=jnp.float32)
    output = from_blocks(out_b.astype(jnp.bfloat16).reshape(nb, row_count, block_size))
    scale = 1.0 / math.sqrt(map_count * lax.axis_size("map") * pix_count * patch_count)
    early = jnp.einsum("krmcp,rmop->kco", terms[:2], cot_b, preferred_element_type=jnp.float32)
    late = jnp.einsum("rmcp,rmop->co", terms[2], cot_b, preferred_element_type=jnp.float32)
    local_grad = jnp.concatenate([early, late[None]])
    filter_grad = butterfly_sum(local_grad, ("patch", "map")) * scale
    return (output, from_blocks(input_grad), filter_grad)


def solution(mesh):
    placed = (
        P("map", None, "patch"),
        P("map", None, "patch"),
        P("patch", None, None, None),
        P("patch", None),
        P(),
    )
    return jax.shard_map(
        per_device,
        mesh=mesh,
        in_specs=placed,
        out_specs=(P("map", None, "patch"), P("map", None, "patch"), P()),
        check_vma=False,
    )
```

```python
import math

import jax
import jax.numpy as jnp
from jax import lax
from jax.sharding import PartitionSpec as P

REACH = 2


def ring_partner(coord, size, level):
    if size == 4 and level == 1:
        return (coord + 1) % size if coord % 2 else (coord - 1) % size
    return coord ^ (1 << level)


def torus_steps(patch_count, map_count):
    def coords(p, m):
        return dict(y=p // 4, x=((p // 2) % 2) * 2 + m // 16, z=m % 16, core=p % 2)

    def linear(c):
        p = c["y"] * 4 + (c["x"] // 2) * 2 + c["core"]
        return p * map_count + (c["x"] % 2) * 16 + c["z"]

    sizes = dict(core=2, x=4, y=4, z=16)
    plan = [("core", 0), ("x", 0), ("x", 1), ("y", 0), ("y", 1), ("z", 0), ("z", 1)]
    steps = []
    for name, level in plan:
        pairs = []
        for p in range(patch_count):
            for m in range(map_count):
                c = coords(p, m)
                d = dict(c)
                d[name] = ring_partner(c[name], sizes[name], level)
                pairs.append((linear(c), linear(d)))
        steps.append(pairs)
    for odd_up in (False, True):
        pairs = []
        for p in range(patch_count):
            for m in range(map_count):
                c = coords(p, m)
                d = dict(c)
                g = c["z"] // 4
                if not odd_up:
                    d["z"] = c["z"] ^ 4
                else:
                    d["z"] = (c["z"] + 4) % 16 if g % 2 else (c["z"] - 4) % 16
                pairs.append((linear(c), linear(d)))
        steps.append(pairs)
    return steps


def butterfly_sum(x, axes):
    patch_count, map_count = (lax.axis_size(a) for a in axes)
    if (patch_count, map_count) == (16, 32):
        for pairs in torus_steps(patch_count, map_count):
            x = x + lax.ppermute(x, axes, pairs)
        return x
    for axis in axes:
        count = lax.axis_size(axis)
        step = 1
        while step < count:
            x = x + lax.ppermute(x, axis, [(i, i ^ step) for i in range(count)])
            step *= 2
    return x


def per_device(maps, cotangent, tiles, columns, filters):
    map_count, chan_count, pix_count = maps.shape
    block_count = tiles.shape[0]
    block_size = tiles.shape[2]
    row_count = map_count * chan_count
    patch_count = lax.axis_size("patch")
    total_blocks = block_count * patch_count
    first_block = lax.axis_index("patch") * block_count
    row_ids = first_block + jnp.arange(block_count, dtype=jnp.int32)
    back_one = ((row_ids - columns[:, 1]) % total_blocks == 1)[:, None, None]
    next_one = ((columns[:, 2] - row_ids) % total_blocks == 1)[:, None, None]
    nb = block_count
    to_right = [(i, (i + 1) % patch_count) for i in range(patch_count)]
    to_left = [((i + 1) % patch_count, i) for i in range(patch_count)]

    def exchange(edge_left, edge_right):
        edge_left, edge_right = lax.optimization_barrier((edge_left, edge_right))
        from_right = lax.ppermute(edge_left, "patch", to_left)
        from_left = lax.ppermute(edge_right, "patch", to_right)
        return from_left, from_right

    def to_blocks(field):
        return field.reshape(row_count, nb, block_size).transpose(1, 0, 2)

    def from_blocks(field):
        return field.transpose(1, 0, 2).reshape(map_count, chan_count, pix_count)

    def forward_local(ext):
        s0 = ext[2 : 2 + nb]
        s1 = jnp.where(back_one, ext[1 : 1 + nb], ext[0:nb])
        s2 = jnp.where(next_one, ext[3 : 3 + nb], ext[4 : 4 + nb])
        picked = jnp.stack([s0, s1, s2], axis=1).astype(jnp.bfloat16)
        return jnp.einsum("rjnq,rjiq->rni", picked, tiles, preferred_element_type=jnp.float32)

    def adjoint_window(grads):
        contrib = jnp.einsum("rni,rjiq->rjnq", grads, tiles, preferred_element_type=jnp.float32)
        c0, c1, c2 = contrib[:, 0], contrib[:, 1], contrib[:, 2]
        zero = jnp.zeros_like(c0)
        pad = lambda v, lo: jnp.pad(v, ((lo, 4 - lo), (0, 0), (0, 0)))
        return (
            pad(c0, 2)
            + pad(jnp.where(back_one, c1, zero), 1)
            + pad(jnp.where(back_one, zero, c1), 0)
            + pad(jnp.where(next_one, c2, zero), 3)
            + pad(jnp.where(next_one, zero, c2), 4)
        )

    x_zero = to_blocks(maps)
    cot_b = to_blocks(cotangent).reshape(nb, map_count, chan_count, block_size)
    cot_split = cotangent.reshape(map_count, chan_count, nb, block_size)
    grads = jnp.einsum("kco,morp->krmcp", filters, cot_split, preferred_element_type=jnp.float32)
    grads = grads.reshape(3, nb, row_count, block_size)
    grad_two = grads[2].astype(jnp.bfloat16)

    win1 = adjoint_window(grad_two)
    x0f = x_zero.astype(jnp.float32)
    map_blocks = maps.reshape(row_count, nb, block_size)
    halo_left = map_blocks[:, 0:2].transpose(1, 0, 2).astype(jnp.float32)
    halo_right = map_blocks[:, nb - 2 : nb].transpose(1, 0, 2).astype(jnp.float32)
    send_left = jnp.stack([halo_left, win1[0:2]])
    send_right = jnp.stack([halo_right, win1[nb + 2 : nb + 4]])
    got_left, got_right = exchange(send_left, send_right)
    ext0 = jnp.concatenate([got_left[0], x0f, got_right[0]], axis=0)
    x_one = forward_local(ext0).astype(jnp.bfloat16)
    adj1 = win1[2 : 2 + nb]
    adj1 = adj1.at[0:2].add(got_left[1])
    adj1 = adj1.at[nb - 2 : nb].add(got_right[1])
    update = (grads[1] + 2.0 * adj1).astype(jnp.bfloat16)

    win2 = adjoint_window(update)
    x1f = x_one.astype(jnp.float32)
    send_left = jnp.stack([x1f[0:2], win2[0:2]])
    send_right = jnp.stack([x1f[nb - 2 : nb], win2[nb + 2 : nb + 4]])
    got_left, got_right = exchange(send_left, send_right)
    ext1 = jnp.concatenate([got_left[0], x1f, got_right[0]], axis=0)
    x_two = (2.0 * forward_local(ext1) - x0f).astype(jnp.bfloat16)
    adj2 = win2[2 : 2 + nb]
    adj2 = adj2.at[0:2].add(got_left[1])
    adj2 = adj2.at[nb - 2 : nb].add(got_right[1])
    input_grad = (grads[0] - grad_two.astype(jnp.float32) + adj2).astype(jnp.bfloat16)

    split = (nb, map_count, chan_count, block_size)
    terms = jnp.stack([x_zero.reshape(split), x_one.reshape(split), x_two.reshape(split)])
    out_b = jnp.einsum("kco,krmcp->rmop", filters, terms, preferred_element_type=jnp.float32)
    output = from_blocks(out_b.astype(jnp.bfloat16).reshape(nb, row_count, block_size))
    scale = 1.0 / math.sqrt(map_count * lax.axis_size("map") * pix_count * patch_count)
    early = jnp.einsum("krmcp,rmop->kco", terms[:2], cot_b, preferred_element_type=jnp.float32)
    late = jnp.einsum("rmcp,rmop->co", terms[2], cot_b, preferred_element_type=jnp.float32)
    local_grad = jnp.concatenate([early, late[None]])
    filter_grad = butterfly_sum(local_grad, ("patch", "map")) * scale
    return (output, from_blocks(input_grad), filter_grad)


def solution(mesh):
    placed = (
        P("map", None, "patch"),
        P("map", None, "patch"),
        P("patch", None, None, None),
        P("patch", None),
        P(),
    )
    return jax.shard_map(
        per_device,
        mesh=mesh,
        in_specs=placed,
        out_specs=(P("map", None, "patch"), P("map", None, "patch"), P()),
        check_vma=False,
    )
```

```python
import math

import jax
import jax.numpy as jnp
from jax import lax
from jax.experimental import pallas as pl
from jax.experimental.pallas import tpu as pltpu
from jax.sharding import PartitionSpec as P

REACH = 2


def ring_partner(coord, size, level):
    if size == 4 and level == 1:
        return (coord + 1) % size if coord % 2 else (coord - 1) % size
    return coord ^ (1 << level)


def torus_steps(patch_count, map_count):
    def coords(p, m):
        return dict(y=p // 4, x=((p // 2) % 2) * 2 + m // 16, z=m % 16, core=p % 2)

    def linear(c):
        p = c["y"] * 4 + (c["x"] // 2) * 2 + c["core"]
        return p * map_count + (c["x"] % 2) * 16 + c["z"]

    sizes = dict(core=2, x=4, y=4, z=16)
    plan = [("core", 0), ("x", 0), ("x", 1), ("y", 0), ("y", 1), ("z", 0), ("z", 1)]
    steps = []
    for name, level in plan:
        pairs = []
        for p in range(patch_count):
            for m in range(map_count):
                c = coords(p, m)
                d = dict(c)
                d[name] = ring_partner(c[name], sizes[name], level)
                pairs.append((linear(c), linear(d)))
        steps.append(pairs)
    for odd_up in (False, True):
        pairs = []
        for p in range(patch_count):
            for m in range(map_count):
                c = coords(p, m)
                d = dict(c)
                g = c["z"] // 4
                if not odd_up:
                    d["z"] = c["z"] ^ 4
                else:
                    d["z"] = (c["z"] + 4) % 16 if g % 2 else (c["z"] - 4) % 16
                pairs.append((linear(c), linear(d)))
        steps.append(pairs)
    return steps


def butterfly_sum(x, axes):
    patch_count, map_count = (lax.axis_size(a) for a in axes)
    if (patch_count, map_count) == (16, 32):
        for pairs in torus_steps(patch_count, map_count):
            x = x + lax.ppermute(x, axes, pairs)
        return x
    for axis in axes:
        count = lax.axis_size(axis)
        step = 1
        while step < count:
            x = x + lax.ppermute(x, axis, [(i, i ^ step) for i in range(count)])
            step *= 2
    return x


def window_kernel(flags_ref, cot_ref, f_ref, tiles_ref, win_ref):
    nb = tiles_ref.shape[0]
    bs = tiles_ref.shape[2]
    win_ref[...] = jnp.zeros(win_ref.shape, win_ref.dtype)
    f = f_ref[...]
    for r in range(nb):
        rows = [
            jnp.dot(f, cot_ref[m, :, r * bs : (r + 1) * bs], preferred_element_type=jnp.float32)
            for m in range(cot_ref.shape[0])
        ]
        g = jnp.concatenate(rows, axis=0).astype(jnp.bfloat16)
        win_ref[r + 2] += jnp.dot(g, tiles_ref[r, 0], preferred_element_type=jnp.float32)
        win_ref[r + flags_ref[r, 0]] += jnp.dot(g, tiles_ref[r, 1], preferred_element_type=jnp.float32)
        win_ref[r + 4 - flags_ref[r, 1]] += jnp.dot(g, tiles_ref[r, 2], preferred_element_type=jnp.float32)

def first_window(flags, cot, f2, tiles):
    nb, bs = tiles.shape[0], tiles.shape[2]
    rows = cot.shape[0] * f2.shape[0]
    return pl.pallas_call(
        window_kernel,
        out_shape=jax.ShapeDtypeStruct((nb + 4, rows, bs), jnp.float32),
        in_specs=[pl.BlockSpec(memory_space=pltpu.SMEM)] + [pl.BlockSpec(memory_space=pltpu.VMEM)] * 3,
        out_specs=pl.BlockSpec(memory_space=pltpu.VMEM),
    )(flags, cot, f2, tiles)


def per_device(maps, cotangent, tiles, columns, filters):
    map_count, chan_count, pix_count = maps.shape
    block_count = tiles.shape[0]
    block_size = tiles.shape[2]
    row_count = map_count * chan_count
    patch_count = lax.axis_size("patch")
    total_blocks = block_count * patch_count
    first_block = lax.axis_index("patch") * block_count
    row_ids = first_block + jnp.arange(block_count, dtype=jnp.int32)
    back_one = ((row_ids - columns[:, 1]) % total_blocks == 1)[:, None, None]
    next_one = ((columns[:, 2] - row_ids) % total_blocks == 1)[:, None, None]
    nb = block_count
    to_right = [(i, (i + 1) % patch_count) for i in range(patch_count)]
    to_left = [((i + 1) % patch_count, i) for i in range(patch_count)]

    def exchange(edge_left, edge_right):
        edge_left, edge_right = lax.optimization_barrier((edge_left, edge_right))
        from_right = lax.ppermute(edge_left, "patch", to_left)
        from_left = lax.ppermute(edge_right, "patch", to_right)
        return from_left, from_right

    def to_blocks(field):
        return field.reshape(row_count, nb, block_size).transpose(1, 0, 2)

    def from_blocks(field):
        return field.transpose(1, 0, 2).reshape(map_count, chan_count, pix_count)

    def forward_local(ext):
        s0 = ext[2 : 2 + nb]
        s1 = jnp.where(back_one, ext[1 : 1 + nb], ext[0:nb])
        s2 = jnp.where(next_one, ext[3 : 3 + nb], ext[4 : 4 + nb])
        picked = jnp.stack([s0, s1, s2], axis=1).astype(jnp.bfloat16)
        return jnp.einsum("rjnq,rjiq->rni", picked, tiles, preferred_element_type=jnp.float32)

    def adjoint_window(grads):
        contrib = jnp.einsum("rni,rjiq->rjnq", grads, tiles, preferred_element_type=jnp.float32)
        c0, c1, c2 = contrib[:, 0], contrib[:, 1], contrib[:, 2]
        zero = jnp.zeros_like(c0)
        pad = lambda v, lo: jnp.pad(v, ((lo, 4 - lo), (0, 0), (0, 0)))
        return (
            pad(c0, 2)
            + pad(jnp.where(back_one, c1, zero), 1)
            + pad(jnp.where(back_one, zero, c1), 0)
            + pad(jnp.where(next_one, c2, zero), 3)
            + pad(jnp.where(next_one, zero, c2), 4)
        )

    x_zero = to_blocks(maps)
    cot_b = to_blocks(cotangent).reshape(nb, map_count, chan_count, block_size)
    grads = jnp.einsum("kco,rmop->krmcp", filters, cot_b, preferred_element_type=jnp.float32)
    grads = grads.reshape(3, nb, row_count, block_size)
    grad_two = grads[2].astype(jnp.bfloat16)

    flags = jnp.stack([back_one[:, 0, 0], next_one[:, 0, 0]], axis=1).astype(jnp.int32)
    win1 = first_window(flags, cotangent, filters[2], tiles)
    x0f = x_zero.astype(jnp.float32)
    send_left = jnp.stack([x0f[0:2], win1[0:2]])
    send_right = jnp.stack([x0f[nb - 2 : nb], win1[nb + 2 : nb + 4]])
    got_left, got_right = exchange(send_left, send_right)
    ext0 = jnp.concatenate([got_left[0], x0f, got_right[0]], axis=0)
    x_one = forward_local(ext0).astype(jnp.bfloat16)
    adj1 = win1[2 : 2 + nb]
    adj1 = adj1.at[0:2].add(got_left[1])
    adj1 = adj1.at[nb - 2 : nb].add(got_right[1])
    update = (grads[1] + 2.0 * adj1).astype(jnp.bfloat16)

    win2 = adjoint_window(update)
    x1f = x_one.astype(jnp.float32)
    send_left = jnp.stack([x1f[0:2], win2[0:2]])
    send_right = jnp.stack([x1f[nb - 2 : nb], win2[nb + 2 : nb + 4]])
    got_left, got_right = exchange(send_left, send_right)
    ext1 = jnp.concatenate([got_left[0], x1f, got_right[0]], axis=0)
    x_two = (2.0 * forward_local(ext1) - x0f).astype(jnp.bfloat16)
    adj2 = win2[2 : 2 + nb]
    adj2 = adj2.at[0:2].add(got_left[1])
    adj2 = adj2.at[nb - 2 : nb].add(got_right[1])
    input_grad = (grads[0] - grad_two.astype(jnp.float32) + adj2).astype(jnp.bfloat16)

    split = (nb, map_count, chan_count, block_size)
    terms = jnp.stack([x_zero.reshape(split), x_one.reshape(split), x_two.reshape(split)])
    out_b = jnp.einsum("kco,krmcp->rmop", filters, terms, preferred_element_type=jnp.float32)
    output = from_blocks(out_b.astype(jnp.bfloat16).reshape(nb, row_count, block_size))
    scale = 1.0 / math.sqrt(map_count * lax.axis_size("map") * pix_count * patch_count)
    early = jnp.einsum("krmcp,rmop->kco", terms[:2], cot_b, preferred_element_type=jnp.float32)
    late = jnp.einsum("rmcp,rmop->co", terms[2], cot_b, preferred_element_type=jnp.float32)
    local_grad = jnp.concatenate([early, late[None]])
    filter_grad = butterfly_sum(local_grad, ("patch", "map")) * scale
    return (output, from_blocks(input_grad), filter_grad)


def solution(mesh):
    placed = (
        P("map", None, "patch"),
        P("map", None, "patch"),
        P("patch", None, None, None),
        P("patch", None),
        P(),
    )
    return jax.shard_map(
        per_device,
        mesh=mesh,
        in_specs=placed,
        out_specs=(P("map", None, "patch"), P("map", None, "patch"), P()),
        check_vma=False,
    )
```

```python
import math

import jax
import jax.numpy as jnp
from jax import lax
from jax.experimental import pallas as pl
from jax.experimental.pallas import tpu as pltpu
from jax.sharding import PartitionSpec as P

REACH = 2


def ring_partner(coord, size, level):
    if size == 4 and level == 1:
        return (coord + 1) % size if coord % 2 else (coord - 1) % size
    return coord ^ (1 << level)


def torus_steps(patch_count, map_count):
    def coords(p, m):
        return dict(y=p // 4, x=((p // 2) % 2) * 2 + m // 16, z=m % 16, core=p % 2)

    def linear(c):
        p = c["y"] * 4 + (c["x"] // 2) * 2 + c["core"]
        return p * map_count + (c["x"] % 2) * 16 + c["z"]

    sizes = dict(core=2, x=4, y=4, z=16)
    plan = [("core", 0), ("x", 0), ("x", 1), ("y", 0), ("y", 1), ("z", 0), ("z", 1)]
    steps = []
    for name, level in plan:
        pairs = []
        for p in range(patch_count):
            for m in range(map_count):
                c = coords(p, m)
                d = dict(c)
                d[name] = ring_partner(c[name], sizes[name], level)
                pairs.append((linear(c), linear(d)))
        steps.append(pairs)
    for odd_up in (False, True):
        pairs = []
        for p in range(patch_count):
            for m in range(map_count):
                c = coords(p, m)
                d = dict(c)
                g = c["z"] // 4
                if not odd_up:
                    d["z"] = c["z"] ^ 4
                else:
                    d["z"] = (c["z"] + 4) % 16 if g % 2 else (c["z"] - 4) % 16
                pairs.append((linear(c), linear(d)))
        steps.append(pairs)
    return steps


def butterfly_sum(x, axes):
    patch_count, map_count = (lax.axis_size(a) for a in axes)
    if (patch_count, map_count) == (16, 32):
        for pairs in torus_steps(patch_count, map_count):
            x = x + lax.ppermute(x, axes, pairs)
        return x
    for axis in axes:
        count = lax.axis_size(axis)
        step = 1
        while step < count:
            x = x + lax.ppermute(x, axis, [(i, i ^ step) for i in range(count)])
            step *= 2
    return x


def window_kernel(flags_ref, cot_ref, maps_ref, f_ref, tiles_ref, win_ref, left_ref, right_ref):
    nb = tiles_ref.shape[0]
    bs = tiles_ref.shape[2]
    maps_per = cot_ref.shape[0]
    win_ref[...] = jnp.zeros(win_ref.shape, win_ref.dtype)
    f = f_ref[2]
    for r in range(nb):
        rows = [
            jnp.dot(f, cot_ref[m, :, r * bs : (r + 1) * bs], preferred_element_type=jnp.float32)
            for m in range(maps_per)
        ]
        g = jnp.concatenate(rows, axis=0).astype(jnp.bfloat16)
        win_ref[r + 2] += jnp.dot(g, tiles_ref[r, 0], preferred_element_type=jnp.float32)
        win_ref[r + flags_ref[r, 0]] += jnp.dot(g, tiles_ref[r, 1], preferred_element_type=jnp.float32)
        win_ref[r + 4 - flags_ref[r, 1]] += jnp.dot(g, tiles_ref[r, 2], preferred_element_type=jnp.float32)

    def map_block(r):
        return jnp.concatenate(
            [maps_ref[m, :, r * bs : (r + 1) * bs] for m in range(maps_per)], axis=0
        ).astype(jnp.float32)

    for i in range(2):
        left_ref[0, i] = map_block(i)
        left_ref[1, i] = win_ref[i]
        right_ref[0, i] = map_block(nb - 2 + i)
        right_ref[1, i] = win_ref[nb + 2 + i]


def first_window(flags, cot, maps, filters, tiles):
    nb, bs = tiles.shape[0], tiles.shape[2]
    rows = cot.shape[0] * cot.shape[1]
    edge = jax.ShapeDtypeStruct((2, 2, rows, bs), jnp.float32)
    vmem = pl.BlockSpec(memory_space=pltpu.VMEM)
    return pl.pallas_call(
        window_kernel,
        out_shape=(jax.ShapeDtypeStruct((nb + 4, rows, bs), jnp.float32), edge, edge),
        in_specs=[pl.BlockSpec(memory_space=pltpu.SMEM)] + [vmem] * 4,
        out_specs=(vmem, vmem, vmem),
    )(flags, cot, maps, filters, tiles)


def per_device(maps, cotangent, tiles, columns, filters):
    map_count, chan_count, pix_count = maps.shape
    block_count = tiles.shape[0]
    block_size = tiles.shape[2]
    row_count = map_count * chan_count
    patch_count = lax.axis_size("patch")
    total_blocks = block_count * patch_count
    first_block = lax.axis_index("patch") * block_count
    row_ids = first_block + jnp.arange(block_count, dtype=jnp.int32)
    back_one = ((row_ids - columns[:, 1]) % total_blocks == 1)[:, None, None]
    next_one = ((columns[:, 2] - row_ids) % total_blocks == 1)[:, None, None]
    nb = block_count
    to_right = [(i, (i + 1) % patch_count) for i in range(patch_count)]
    to_left = [((i + 1) % patch_count, i) for i in range(patch_count)]

    def exchange(edge_left, edge_right):
        edge_left, edge_right = lax.optimization_barrier((edge_left, edge_right))
        from_right = lax.ppermute(edge_left, "patch", to_left)
        from_left = lax.ppermute(edge_right, "patch", to_right)
        return from_left, from_right

    def to_blocks(field):
        return field.reshape(row_count, nb, block_size).transpose(1, 0, 2)

    def from_blocks(field):
        return field.transpose(1, 0, 2).reshape(map_count, chan_count, pix_count)

    def forward_local(ext):
        s0 = ext[2 : 2 + nb]
        s1 = jnp.where(back_one, ext[1 : 1 + nb], ext[0:nb])
        s2 = jnp.where(next_one, ext[3 : 3 + nb], ext[4 : 4 + nb])
        picked = jnp.stack([s0, s1, s2], axis=1).astype(jnp.bfloat16)
        return jnp.einsum("rjnq,rjiq->rni", picked, tiles, preferred_element_type=jnp.float32)

    def adjoint_window(grads):
        contrib = jnp.einsum("rni,rjiq->rjnq", grads, tiles, preferred_element_type=jnp.float32)
        c0, c1, c2 = contrib[:, 0], contrib[:, 1], contrib[:, 2]
        zero = jnp.zeros_like(c0)
        pad = lambda v, lo: jnp.pad(v, ((lo, 4 - lo), (0, 0), (0, 0)))
        return (
            pad(c0, 2)
            + pad(jnp.where(back_one, c1, zero), 1)
            + pad(jnp.where(back_one, zero, c1), 0)
            + pad(jnp.where(next_one, c2, zero), 3)
            + pad(jnp.where(next_one, zero, c2), 4)
        )

    x_zero = to_blocks(maps)
    cot_b = to_blocks(cotangent).reshape(nb, map_count, chan_count, block_size)
    grads = jnp.einsum("kco,rmop->krmcp", filters, cot_b, preferred_element_type=jnp.float32)
    grads = grads.reshape(3, nb, row_count, block_size)
    grad_two = grads[2].astype(jnp.bfloat16)

    flags = jnp.stack([back_one[:, 0, 0], next_one[:, 0, 0]], axis=1).astype(jnp.int32)
    win1, send_left, send_right = first_window(flags, cotangent, maps, filters, tiles)
    x0f = x_zero.astype(jnp.float32)
    got_left, got_right = exchange(send_left, send_right)
    ext0 = jnp.concatenate([got_left[0], x0f, got_right[0]], axis=0)
    x_one = forward_local(ext0).astype(jnp.bfloat16)
    adj1 = win1[2 : 2 + nb]
    adj1 = adj1.at[0:2].add(got_left[1])
    adj1 = adj1.at[nb - 2 : nb].add(got_right[1])
    update = (grads[1] + 2.0 * adj1).astype(jnp.bfloat16)

    win2 = adjoint_window(update)
    x1f = x_one.astype(jnp.float32)
    send_left = jnp.stack([x1f[0:2], win2[0:2]])
    send_right = jnp.stack([x1f[nb - 2 : nb], win2[nb + 2 : nb + 4]])
    got_left, got_right = exchange(send_left, send_right)
    ext1 = jnp.concatenate([got_left[0], x1f, got_right[0]], axis=0)
    x_two = (2.0 * forward_local(ext1) - x0f).astype(jnp.bfloat16)
    adj2 = win2[2 : 2 + nb]
    adj2 = adj2.at[0:2].add(got_left[1])
    adj2 = adj2.at[nb - 2 : nb].add(got_right[1])
    input_grad = (grads[0] - grad_two.astype(jnp.float32) + adj2).astype(jnp.bfloat16)

    split = (nb, map_count, chan_count, block_size)
    terms = jnp.stack([x_zero.reshape(split), x_one.reshape(split), x_two.reshape(split)])
    out_b = jnp.einsum("kco,krmcp->rmop", filters, terms, preferred_element_type=jnp.float32)
    output = from_blocks(out_b.astype(jnp.bfloat16).reshape(nb, row_count, block_size))
    scale = 1.0 / math.sqrt(map_count * lax.axis_size("map") * pix_count * patch_count)
    early = jnp.einsum("krmcp,rmop->kco", terms[:2], cot_b, preferred_element_type=jnp.float32)
    late = jnp.einsum("rmcp,rmop->co", terms[2], cot_b, preferred_element_type=jnp.float32)
    local_grad = jnp.concatenate([early, late[None]])
    filter_grad = butterfly_sum(local_grad, ("patch", "map")) * scale
    return (output, from_blocks(input_grad), filter_grad)


def solution(mesh):
    placed = (
        P("map", None, "patch"),
        P("map", None, "patch"),
        P("patch", None, None, None),
        P("patch", None),
        P(),
    )
    return jax.shard_map(
        per_device,
        mesh=mesh,
        in_specs=placed,
        out_specs=(P("map", None, "patch"), P("map", None, "patch"), P()),
        check_vma=False,
    )
```

```python
import math

import jax
import jax.numpy as jnp
from jax import lax
from jax.experimental import pallas as pl
from jax.experimental.pallas import tpu as pltpu
from jax.sharding import PartitionSpec as P

REACH = 2


def ring_partner(coord, size, level):
    if size == 4 and level == 1:
        return (coord + 1) % size if coord % 2 else (coord - 1) % size
    return coord ^ (1 << level)


def torus_steps(patch_count, map_count):
    def coords(p, m):
        return dict(y=p // 4, x=((p // 2) % 2) * 2 + m // 16, z=m % 16, core=p % 2)

    def linear(c):
        p = c["y"] * 4 + (c["x"] // 2) * 2 + c["core"]
        return p * map_count + (c["x"] % 2) * 16 + c["z"]

    sizes = dict(core=2, x=4, y=4, z=16)
    plan = [("core", 0), ("x", 0), ("x", 1), ("y", 0), ("y", 1), ("z", 0), ("z", 1)]
    steps = []
    for name, level in plan:
        pairs = []
        for p in range(patch_count):
            for m in range(map_count):
                c = coords(p, m)
                d = dict(c)
                d[name] = ring_partner(c[name], sizes[name], level)
                pairs.append((linear(c), linear(d)))
        steps.append(pairs)
    for odd_up in (False, True):
        pairs = []
        for p in range(patch_count):
            for m in range(map_count):
                c = coords(p, m)
                d = dict(c)
                g = c["z"] // 4
                if not odd_up:
                    d["z"] = c["z"] ^ 4
                else:
                    d["z"] = (c["z"] + 4) % 16 if g % 2 else (c["z"] - 4) % 16
                pairs.append((linear(c), linear(d)))
        steps.append(pairs)
    return steps


def butterfly_sum(x, axes):
    patch_count, map_count = (lax.axis_size(a) for a in axes)
    if (patch_count, map_count) == (16, 32):
        for pairs in torus_steps(patch_count, map_count):
            x = x + lax.ppermute(x, axes, pairs)
        return x
    for axis in axes:
        count = lax.axis_size(axis)
        step = 1
        while step < count:
            x = x + lax.ppermute(x, axis, [(i, i ^ step) for i in range(count)])
            step *= 2
    return x


def window_kernel(flags_ref, cot_ref, f_ref, tiles_ref, win_ref):
    nb = tiles_ref.shape[0]
    bs = tiles_ref.shape[2]
    win_ref[...] = jnp.zeros(win_ref.shape, win_ref.dtype)
    f = f_ref[2]
    for r in range(nb):
        rows = [
            jnp.dot(f, cot_ref[m, :, r * bs : (r + 1) * bs], preferred_element_type=jnp.float32)
            for m in range(cot_ref.shape[0])
        ]
        g = jnp.concatenate(rows, axis=0).astype(jnp.bfloat16)
        win_ref[r + 2] += jnp.dot(g, tiles_ref[r, 0], preferred_element_type=jnp.float32)
        win_ref[r + flags_ref[r, 0]] += jnp.dot(g, tiles_ref[r, 1], preferred_element_type=jnp.float32)
        win_ref[r + 4 - flags_ref[r, 1]] += jnp.dot(g, tiles_ref[r, 2], preferred_element_type=jnp.float32)

def first_window(flags, cot, f2, tiles):
    nb, bs = tiles.shape[0], tiles.shape[2]
    rows = cot.shape[0] * f2.shape[1]
    return pl.pallas_call(
        window_kernel,
        out_shape=jax.ShapeDtypeStruct((nb + 4, rows, bs), jnp.float32),
        in_specs=[pl.BlockSpec(memory_space=pltpu.SMEM)] + [pl.BlockSpec(memory_space=pltpu.VMEM)] * 3,
        out_specs=pl.BlockSpec(memory_space=pltpu.VMEM),
    )(flags, cot, f2, tiles)


def per_device(maps, cotangent, tiles, columns, filters):
    map_count, chan_count, pix_count = maps.shape
    block_count = tiles.shape[0]
    block_size = tiles.shape[2]
    row_count = map_count * chan_count
    patch_count = lax.axis_size("patch")
    total_blocks = block_count * patch_count
    first_block = lax.axis_index("patch") * block_count
    row_ids = first_block + jnp.arange(block_count, dtype=jnp.int32)
    back_one = ((row_ids - columns[:, 1]) % total_blocks == 1)[:, None, None]
    next_one = ((columns[:, 2] - row_ids) % total_blocks == 1)[:, None, None]
    nb = block_count
    to_right = [(i, (i + 1) % patch_count) for i in range(patch_count)]
    to_left = [((i + 1) % patch_count, i) for i in range(patch_count)]

    def exchange(edge_left, edge_right):
        edge_left, edge_right = lax.optimization_barrier((edge_left, edge_right))
        from_right = lax.ppermute(edge_left, "patch", to_left)
        from_left = lax.ppermute(edge_right, "patch", to_right)
        return from_left, from_right

    def to_blocks(field):
        return field.reshape(row_count, nb, block_size).transpose(1, 0, 2)

    def from_blocks(field):
        return field.transpose(1, 0, 2).reshape(map_count, chan_count, pix_count)

    def forward_local(ext):
        s0 = ext[2 : 2 + nb]
        s1 = jnp.where(back_one, ext[1 : 1 + nb], ext[0:nb])
        s2 = jnp.where(next_one, ext[3 : 3 + nb], ext[4 : 4 + nb])
        picked = jnp.stack([s0, s1, s2], axis=1).astype(jnp.bfloat16)
        return jnp.einsum("rjnq,rjiq->rni", picked, tiles, preferred_element_type=jnp.float32)

    def adjoint_window(grads):
        contrib = jnp.einsum("rni,rjiq->rjnq", grads, tiles, preferred_element_type=jnp.float32)
        c0, c1, c2 = contrib[:, 0], contrib[:, 1], contrib[:, 2]
        zero = jnp.zeros_like(c0)
        pad = lambda v, lo: jnp.pad(v, ((lo, 4 - lo), (0, 0), (0, 0)))
        return (
            pad(c0, 2)
            + pad(jnp.where(back_one, c1, zero), 1)
            + pad(jnp.where(back_one, zero, c1), 0)
            + pad(jnp.where(next_one, c2, zero), 3)
            + pad(jnp.where(next_one, zero, c2), 4)
        )

    x_zero = to_blocks(maps)
    cot_b = to_blocks(cotangent).reshape(nb, map_count, chan_count, block_size)
    grads = jnp.einsum("kco,rmop->krmcp", filters, cot_b, preferred_element_type=jnp.float32)
    grads = grads.reshape(3, nb, row_count, block_size)
    grad_two = grads[2].astype(jnp.bfloat16)

    flags = jnp.stack([back_one[:, 0, 0], next_one[:, 0, 0]], axis=1).astype(jnp.int32)
    win1 = first_window(flags, cotangent, filters, tiles)
    x0f = x_zero.astype(jnp.float32)
    send_left = jnp.stack([x0f[0:2], win1[0:2]])
    send_right = jnp.stack([x0f[nb - 2 : nb], win1[nb + 2 : nb + 4]])
    got_left, got_right = exchange(send_left, send_right)
    ext0 = jnp.concatenate([got_left[0], x0f, got_right[0]], axis=0)
    x_one = forward_local(ext0).astype(jnp.bfloat16)
    adj1 = win1[2 : 2 + nb]
    adj1 = adj1.at[0:2].add(got_left[1])
    adj1 = adj1.at[nb - 2 : nb].add(got_right[1])
    update = (grads[1] + 2.0 * adj1).astype(jnp.bfloat16)

    win2 = adjoint_window(update)
    x1f = x_one.astype(jnp.float32)
    send_left = jnp.stack([x1f[0:2], win2[0:2]])
    send_right = jnp.stack([x1f[nb - 2 : nb], win2[nb + 2 : nb + 4]])
    got_left, got_right = exchange(send_left, send_right)
    ext1 = jnp.concatenate([got_left[0], x1f, got_right[0]], axis=0)
    x_two = (2.0 * forward_local(ext1) - x0f).astype(jnp.bfloat16)
    adj2 = win2[2 : 2 + nb]
    adj2 = adj2.at[0:2].add(got_left[1])
    adj2 = adj2.at[nb - 2 : nb].add(got_right[1])
    input_grad = (grads[0] - grad_two.astype(jnp.float32) + adj2).astype(jnp.bfloat16)

    split = (nb, map_count, chan_count, block_size)
    terms = jnp.stack([x_zero.reshape(split), x_one.reshape(split), x_two.reshape(split)])
    out_b = jnp.einsum("kco,krmcp->rmop", filters, terms, preferred_element_type=jnp.float32)
    output = from_blocks(out_b.astype(jnp.bfloat16).reshape(nb, row_count, block_size))
    scale = 1.0 / math.sqrt(map_count * lax.axis_size("map") * pix_count * patch_count)
    early = jnp.einsum("krmcp,rmop->kco", terms[:2], cot_b, preferred_element_type=jnp.float32)
    late = jnp.einsum("rmcp,rmop->co", terms[2], cot_b, preferred_element_type=jnp.float32)
    local_grad = jnp.concatenate([early, late[None]])
    filter_grad = butterfly_sum(local_grad, ("patch", "map")) * scale
    return (output, from_blocks(input_grad), filter_grad)


def solution(mesh):
    placed = (
        P("map", None, "patch"),
        P("map", None, "patch"),
        P("patch", None, None, None),
        P("patch", None),
        P(),
    )
    return jax.shard_map(
        per_device,
        mesh=mesh,
        in_specs=placed,
        out_specs=(P("map", None, "patch"), P("map", None, "patch"), P()),
        check_vma=False,
    )
```

```python
import functools
import math

import jax
import jax.numpy as jnp
from jax import lax
from jax.experimental import pallas as pl
from jax.experimental.pallas import tpu as pltpu
from jax.sharding import PartitionSpec as P

REACH = 2


def ring_partner(coord, size, level):
    if size == 4 and level == 1:
        return (coord + 1) % size if coord % 2 else (coord - 1) % size
    return coord ^ (1 << level)


def torus_steps(patch_count, map_count):
    def coords(p, m):
        return dict(y=p // 4, x=((p // 2) % 2) * 2 + m // 16, z=m % 16, core=p % 2)

    def linear(c):
        p = c["y"] * 4 + (c["x"] // 2) * 2 + c["core"]
        return p * map_count + (c["x"] % 2) * 16 + c["z"]

    sizes = dict(core=2, x=4, y=4, z=16)
    plan = [("core", 0), ("x", 0), ("x", 1), ("y", 0), ("y", 1), ("z", 0), ("z", 1)]
    steps = []
    for name, level in plan:
        pairs = []
        for p in range(patch_count):
            for m in range(map_count):
                c = coords(p, m)
                d = dict(c)
                d[name] = ring_partner(c[name], sizes[name], level)
                pairs.append((linear(c), linear(d)))
        steps.append(pairs)
    for odd_up in (False, True):
        pairs = []
        for p in range(patch_count):
            for m in range(map_count):
                c = coords(p, m)
                d = dict(c)
                g = c["z"] // 4
                if not odd_up:
                    d["z"] = c["z"] ^ 4
                else:
                    d["z"] = (c["z"] + 4) % 16 if g % 2 else (c["z"] - 4) % 16
                pairs.append((linear(c), linear(d)))
        steps.append(pairs)
    return steps


def butterfly_sum(x, axes):
    patch_count, map_count = (lax.axis_size(a) for a in axes)
    if (patch_count, map_count) == (16, 32):
        for pairs in torus_steps(patch_count, map_count):
            x = x + lax.ppermute(x, axes, pairs)
        return x
    for axis in axes:
        count = lax.axis_size(axis)
        step = 1
        while step < count:
            x = x + lax.ppermute(x, axis, [(i, i ^ step) for i in range(count)])
            step *= 2
    return x


def window_kernel(total_blocks, cols_ref, cot_ref, f_ref, tiles_ref, win_ref):
    nb = tiles_ref.shape[0]
    bs = tiles_ref.shape[2]
    win_ref[...] = jnp.zeros(win_ref.shape, win_ref.dtype)
    f = f_ref[2]
    for r in range(nb):
        rows = [
            jnp.dot(f, cot_ref[m, :, r * bs : (r + 1) * bs], preferred_element_type=jnp.float32)
            for m in range(cot_ref.shape[0])
        ]
        g = jnp.concatenate(rows, axis=0).astype(jnp.bfloat16)
        win_ref[r + 2] += jnp.dot(g, tiles_ref[r, 0], preferred_element_type=jnp.float32)
        row = lax.axis_index("patch") * nb + r
        back = row - cols_ref[r, 1]
        back = jnp.where(back < 0, back + total_blocks, back)
        ahead = cols_ref[r, 2] - row
        ahead = jnp.where(ahead < 0, ahead + total_blocks, ahead)
        back_one = (back == 1).astype(jnp.int32)
        next_one = (ahead == 1).astype(jnp.int32)
        win_ref[r + back_one] += jnp.dot(g, tiles_ref[r, 1], preferred_element_type=jnp.float32)
        win_ref[r + 4 - next_one] += jnp.dot(g, tiles_ref[r, 2], preferred_element_type=jnp.float32)

def first_window(columns, cot, f2, tiles):
    nb, bs = tiles.shape[0], tiles.shape[2]
    rows = cot.shape[0] * f2.shape[1]
    total_blocks = nb * lax.axis_size("patch")
    return pl.pallas_call(
        functools.partial(window_kernel, total_blocks),
        out_shape=jax.ShapeDtypeStruct((nb + 4, rows, bs), jnp.float32),
        in_specs=[pl.BlockSpec(memory_space=pltpu.SMEM)] + [pl.BlockSpec(memory_space=pltpu.VMEM)] * 3,
        out_specs=pl.BlockSpec(memory_space=pltpu.VMEM),
    )(columns, cot, f2, tiles)


def per_device(maps, cotangent, tiles, columns, filters):
    map_count, chan_count, pix_count = maps.shape
    block_count = tiles.shape[0]
    block_size = tiles.shape[2]
    row_count = map_count * chan_count
    patch_count = lax.axis_size("patch")
    total_blocks = block_count * patch_count
    first_block = lax.axis_index("patch") * block_count
    row_ids = first_block + jnp.arange(block_count, dtype=jnp.int32)
    back_one = ((row_ids - columns[:, 1]) % total_blocks == 1)[:, None, None]
    next_one = ((columns[:, 2] - row_ids) % total_blocks == 1)[:, None, None]
    nb = block_count
    to_right = [(i, (i + 1) % patch_count) for i in range(patch_count)]
    to_left = [((i + 1) % patch_count, i) for i in range(patch_count)]

    def exchange(edge_left, edge_right):
        edge_left, edge_right = lax.optimization_barrier((edge_left, edge_right))
        from_right = lax.ppermute(edge_left, "patch", to_left)
        from_left = lax.ppermute(edge_right, "patch", to_right)
        return from_left, from_right

    def to_blocks(field):
        return field.reshape(row_count, nb, block_size).transpose(1, 0, 2)

    def from_blocks(field):
        return field.transpose(1, 0, 2).reshape(map_count, chan_count, pix_count)

    def forward_local(ext):
        s0 = ext[2 : 2 + nb]
        s1 = jnp.where(back_one, ext[1 : 1 + nb], ext[0:nb])
        s2 = jnp.where(next_one, ext[3 : 3 + nb], ext[4 : 4 + nb])
        picked = jnp.stack([s0, s1, s2], axis=1).astype(jnp.bfloat16)
        return jnp.einsum("rjnq,rjiq->rni", picked, tiles, preferred_element_type=jnp.float32)

    def adjoint_window(grads):
        contrib = jnp.einsum("rni,rjiq->rjnq", grads, tiles, preferred_element_type=jnp.float32)
        c0, c1, c2 = contrib[:, 0], contrib[:, 1], contrib[:, 2]
        zero = jnp.zeros_like(c0)
        pad = lambda v, lo: jnp.pad(v, ((lo, 4 - lo), (0, 0), (0, 0)))
        return (
            pad(c0, 2)
            + pad(jnp.where(back_one, c1, zero), 1)
            + pad(jnp.where(back_one, zero, c1), 0)
            + pad(jnp.where(next_one, c2, zero), 3)
            + pad(jnp.where(next_one, zero, c2), 4)
        )

    x_zero = to_blocks(maps)
    cot_b = to_blocks(cotangent).reshape(nb, map_count, chan_count, block_size)
    grads = jnp.einsum("kco,rmop->krmcp", filters, cot_b, preferred_element_type=jnp.float32)
    grads = grads.reshape(3, nb, row_count, block_size)
    grad_two = grads[2].astype(jnp.bfloat16)

    win1 = first_window(columns, cotangent, filters, tiles)
    x0f = x_zero.astype(jnp.float32)
    send_left = jnp.stack([x0f[0:2], win1[0:2]])
    send_right = jnp.stack([x0f[nb - 2 : nb], win1[nb + 2 : nb + 4]])
    got_left, got_right = exchange(send_left, send_right)
    ext0 = jnp.concatenate([got_left[0], x0f, got_right[0]], axis=0)
    x_one = forward_local(ext0).astype(jnp.bfloat16)
    adj1 = win1[2 : 2 + nb]
    adj1 = adj1.at[0:2].add(got_left[1])
    adj1 = adj1.at[nb - 2 : nb].add(got_right[1])
    update = (grads[1] + 2.0 * adj1).astype(jnp.bfloat16)

    win2 = adjoint_window(update)
    x1f = x_one.astype(jnp.float32)
    send_left = jnp.stack([x1f[0:2], win2[0:2]])
    send_right = jnp.stack([x1f[nb - 2 : nb], win2[nb + 2 : nb + 4]])
    got_left, got_right = exchange(send_left, send_right)
    ext1 = jnp.concatenate([got_left[0], x1f, got_right[0]], axis=0)
    x_two = (2.0 * forward_local(ext1) - x0f).astype(jnp.bfloat16)
    adj2 = win2[2 : 2 + nb]
    adj2 = adj2.at[0:2].add(got_left[1])
    adj2 = adj2.at[nb - 2 : nb].add(got_right[1])
    input_grad = (grads[0] - grad_two.astype(jnp.float32) + adj2).astype(jnp.bfloat16)

    split = (nb, map_count, chan_count, block_size)
    terms = jnp.stack([x_zero.reshape(split), x_one.reshape(split), x_two.reshape(split)])
    out_b = jnp.einsum("kco,krmcp->rmop", filters, terms, preferred_element_type=jnp.float32)
    output = from_blocks(out_b.astype(jnp.bfloat16).reshape(nb, row_count, block_size))
    scale = 1.0 / math.sqrt(map_count * lax.axis_size("map") * pix_count * patch_count)
    early = jnp.einsum("krmcp,rmop->kco", terms[:2], cot_b, preferred_element_type=jnp.float32)
    late = jnp.einsum("rmcp,rmop->co", terms[2], cot_b, preferred_element_type=jnp.float32)
    local_grad = jnp.concatenate([early, late[None]])
    filter_grad = butterfly_sum(local_grad, ("patch", "map")) * scale
    return (output, from_blocks(input_grad), filter_grad)


def solution(mesh):
    placed = (
        P("map", None, "patch"),
        P("map", None, "patch"),
        P("patch", None, None, None),
        P("patch", None),
        P(),
    )
    return jax.shard_map(
        per_device,
        mesh=mesh,
        in_specs=placed,
        out_specs=(P("map", None, "patch"), P("map", None, "patch"), P()),
        check_vma=False,
    )
```

```python
import math

import jax
import jax.numpy as jnp
from jax import lax
from jax.experimental import pallas as pl
from jax.experimental.pallas import tpu as pltpu
from jax.sharding import PartitionSpec as P

REACH = 2


def ring_partner(coord, size, level):
    if size == 4 and level == 1:
        return (coord + 1) % size if coord % 2 else (coord - 1) % size
    return coord ^ (1 << level)


def torus_steps(patch_count, map_count):
    def coords(p, m):
        return dict(y=p // 4, x=((p // 2) % 2) * 2 + m // 16, z=m % 16, core=p % 2)

    def linear(c):
        p = c["y"] * 4 + (c["x"] // 2) * 2 + c["core"]
        return p * map_count + (c["x"] % 2) * 16 + c["z"]

    sizes = dict(core=2, x=4, y=4, z=16)
    plan = [("core", 0), ("x", 0), ("x", 1), ("y", 0), ("y", 1), ("z", 0), ("z", 1)]
    steps = []
    for name, level in plan:
        pairs = []
        for p in range(patch_count):
            for m in range(map_count):
                c = coords(p, m)
                d = dict(c)
                d[name] = ring_partner(c[name], sizes[name], level)
                pairs.append((linear(c), linear(d)))
        steps.append(pairs)
    for odd_up in (False, True):
        pairs = []
        for p in range(patch_count):
            for m in range(map_count):
                c = coords(p, m)
                d = dict(c)
                g = c["z"] // 4
                if not odd_up:
                    d["z"] = c["z"] ^ 4
                else:
                    d["z"] = (c["z"] + 4) % 16 if g % 2 else (c["z"] - 4) % 16
                pairs.append((linear(c), linear(d)))
        steps.append(pairs)
    return steps


def butterfly_sum(x, axes):
    patch_count, map_count = (lax.axis_size(a) for a in axes)
    if (patch_count, map_count) == (16, 32):
        for pairs in torus_steps(patch_count, map_count):
            x = x + lax.ppermute(x, axes, pairs)
        return x
    for axis in axes:
        count = lax.axis_size(axis)
        step = 1
        while step < count:
            x = x + lax.ppermute(x, axis, [(i, i ^ step) for i in range(count)])
            step *= 2
    return x


def window_kernel(flags_ref, cot_ref, f_ref, tiles_ref, win_ref):
    r = pl.program_id(0)
    bs = tiles_ref.shape[2]

    @pl.when(r == 0)
    def _():
        win_ref[...] = jnp.zeros(win_ref.shape, win_ref.dtype)

    f = f_ref[2]
    cols = pl.ds(pl.multiple_of(r * bs, bs), bs)
    rows = [
        jnp.dot(f, cot_ref[m, :, cols], preferred_element_type=jnp.float32)
        for m in range(cot_ref.shape[0])
    ]
    g = jnp.concatenate(rows, axis=0).astype(jnp.bfloat16)
    win_ref[r + 2] += jnp.dot(g, tiles_ref[0, 0], preferred_element_type=jnp.float32)
    win_ref[r + flags_ref[r, 0]] += jnp.dot(g, tiles_ref[0, 1], preferred_element_type=jnp.float32)
    win_ref[r + 4 - flags_ref[r, 1]] += jnp.dot(g, tiles_ref[0, 2], preferred_element_type=jnp.float32)


def first_window(flags, cot, f2, tiles):
    nb, slots, bs = tiles.shape[0], tiles.shape[1], tiles.shape[2]
    rows = cot.shape[0] * f2.shape[1]
    whole = lambda shape: pl.BlockSpec(shape, lambda r: (0,) * len(shape))
    return pl.pallas_call(
        window_kernel,
        grid=(nb,),
        out_shape=jax.ShapeDtypeStruct((nb + 4, rows, bs), jnp.float32),
        in_specs=[
            pl.BlockSpec(memory_space=pltpu.SMEM),
            whole(cot.shape),
            whole(f2.shape),
            pl.BlockSpec((1, slots, bs, bs), lambda r: (r, 0, 0, 0)),
        ],
        out_specs=whole((nb + 4, rows, bs)),
    )(flags, cot, f2, tiles)


def per_device(maps, cotangent, tiles, columns, filters):
    map_count, chan_count, pix_count = maps.shape
    block_count = tiles.shape[0]
    block_size = tiles.shape[2]
    row_count = map_count * chan_count
    patch_count = lax.axis_size("patch")
    total_blocks = block_count * patch_count
    first_block = lax.axis_index("patch") * block_count
    row_ids = first_block + jnp.arange(block_count, dtype=jnp.int32)
    back_one = ((row_ids - columns[:, 1]) % total_blocks == 1)[:, None, None]
    next_one = ((columns[:, 2] - row_ids) % total_blocks == 1)[:, None, None]
    nb = block_count
    to_right = [(i, (i + 1) % patch_count) for i in range(patch_count)]
    to_left = [((i + 1) % patch_count, i) for i in range(patch_count)]

    def exchange(edge_left, edge_right):
        edge_left, edge_right = lax.optimization_barrier((edge_left, edge_right))
        from_right = lax.ppermute(edge_left, "patch", to_left)
        from_left = lax.ppermute(edge_right, "patch", to_right)
        return from_left, from_right

    def to_blocks(field):
        return field.reshape(row_count, nb, block_size).transpose(1, 0, 2)

    def from_blocks(field):
        return field.transpose(1, 0, 2).reshape(map_count, chan_count, pix_count)

    def forward_local(ext):
        s0 = ext[2 : 2 + nb]
        s1 = jnp.where(back_one, ext[1 : 1 + nb], ext[0:nb])
        s2 = jnp.where(next_one, ext[3 : 3 + nb], ext[4 : 4 + nb])
        picked = jnp.stack([s0, s1, s2], axis=1).astype(jnp.bfloat16)
        return jnp.einsum("rjnq,rjiq->rni", picked, tiles, preferred_element_type=jnp.float32)

    def adjoint_window(grads):
        contrib = jnp.einsum("rni,rjiq->rjnq", grads, tiles, preferred_element_type=jnp.float32)
        c0, c1, c2 = contrib[:, 0], contrib[:, 1], contrib[:, 2]
        zero = jnp.zeros_like(c0)
        pad = lambda v, lo: jnp.pad(v, ((lo, 4 - lo), (0, 0), (0, 0)))
        return (
            pad(c0, 2)
            + pad(jnp.where(back_one, c1, zero), 1)
            + pad(jnp.where(back_one, zero, c1), 0)
            + pad(jnp.where(next_one, c2, zero), 3)
            + pad(jnp.where(next_one, zero, c2), 4)
        )

    x_zero = to_blocks(maps)
    cot_b = to_blocks(cotangent).reshape(nb, map_count, chan_count, block_size)
    grads = jnp.einsum("kco,rmop->krmcp", filters, cot_b, preferred_element_type=jnp.float32)
    grads = grads.reshape(3, nb, row_count, block_size)
    grad_two = grads[2].astype(jnp.bfloat16)

    flags = jnp.stack([back_one[:, 0, 0], next_one[:, 0, 0]], axis=1).astype(jnp.int32)
    win1 = first_window(flags, cotangent, filters, tiles)
    x0f = x_zero.astype(jnp.float32)
    send_left = jnp.stack([x0f[0:2], win1[0:2]])
    send_right = jnp.stack([x0f[nb - 2 : nb], win1[nb + 2 : nb + 4]])
    got_left, got_right = exchange(send_left, send_right)
    ext0 = jnp.concatenate([got_left[0], x0f, got_right[0]], axis=0)
    x_one = forward_local(ext0).astype(jnp.bfloat16)
    adj1 = win1[2 : 2 + nb]
    adj1 = adj1.at[0:2].add(got_left[1])
    adj1 = adj1.at[nb - 2 : nb].add(got_right[1])
    update = (grads[1] + 2.0 * adj1).astype(jnp.bfloat16)

    win2 = adjoint_window(update)
    x1f = x_one.astype(jnp.float32)
    send_left = jnp.stack([x1f[0:2], win2[0:2]])
    send_right = jnp.stack([x1f[nb - 2 : nb], win2[nb + 2 : nb + 4]])
    got_left, got_right = exchange(send_left, send_right)
    ext1 = jnp.concatenate([got_left[0], x1f, got_right[0]], axis=0)
    x_two = (2.0 * forward_local(ext1) - x0f).astype(jnp.bfloat16)
    adj2 = win2[2 : 2 + nb]
    adj2 = adj2.at[0:2].add(got_left[1])
    adj2 = adj2.at[nb - 2 : nb].add(got_right[1])
    input_grad = (grads[0] - grad_two.astype(jnp.float32) + adj2).astype(jnp.bfloat16)

    split = (nb, map_count, chan_count, block_size)
    terms = jnp.stack([x_zero.reshape(split), x_one.reshape(split), x_two.reshape(split)])
    out_b = jnp.einsum("kco,krmcp->rmop", filters, terms, preferred_element_type=jnp.float32)
    output = from_blocks(out_b.astype(jnp.bfloat16).reshape(nb, row_count, block_size))
    scale = 1.0 / math.sqrt(map_count * lax.axis_size("map") * pix_count * patch_count)
    early = jnp.einsum("krmcp,rmop->kco", terms[:2], cot_b, preferred_element_type=jnp.float32)
    late = jnp.einsum("rmcp,rmop->co", terms[2], cot_b, preferred_element_type=jnp.float32)
    local_grad = jnp.concatenate([early, late[None]])
    filter_grad = butterfly_sum(local_grad, ("patch", "map")) * scale
    return (output, from_blocks(input_grad), filter_grad)


def solution(mesh):
    placed = (
        P("map", None, "patch"),
        P("map", None, "patch"),
        P("patch", None, None, None),
        P("patch", None),
        P(),
    )
    return jax.shard_map(
        per_device,
        mesh=mesh,
        in_specs=placed,
        out_specs=(P("map", None, "patch"), P("map", None, "patch"), P()),
        check_vma=False,
    )
```

```python
import functools
import math

import jax
import jax.numpy as jnp
from jax import lax
from jax.experimental import pallas as pl
from jax.experimental.pallas import tpu as pltpu
from jax.sharding import PartitionSpec as P

REACH = 2


def ring_partner(coord, size, level):
    if size == 4 and level == 1:
        return (coord + 1) % size if coord % 2 else (coord - 1) % size
    return coord ^ (1 << level)


def torus_steps(patch_count, map_count):
    def coords(p, m):
        return dict(y=p // 4, x=((p // 2) % 2) * 2 + m // 16, z=m % 16, core=p % 2)

    def linear(c):
        p = c["y"] * 4 + (c["x"] // 2) * 2 + c["core"]
        return p * map_count + (c["x"] % 2) * 16 + c["z"]

    sizes = dict(core=2, x=4, y=4, z=16)
    plan = [("core", 0), ("x", 0), ("x", 1), ("y", 0), ("y", 1), ("z", 0), ("z", 1)]
    steps = []
    for name, level in plan:
        pairs = []
        for p in range(patch_count):
            for m in range(map_count):
                c = coords(p, m)
                d = dict(c)
                d[name] = ring_partner(c[name], sizes[name], level)
                pairs.append((linear(c), linear(d)))
        steps.append(pairs)
    for odd_up in (False, True):
        pairs = []
        for p in range(patch_count):
            for m in range(map_count):
                c = coords(p, m)
                d = dict(c)
                g = c["z"] // 4
                if not odd_up:
                    d["z"] = c["z"] ^ 4
                else:
                    d["z"] = (c["z"] + 4) % 16 if g % 2 else (c["z"] - 4) % 16
                pairs.append((linear(c), linear(d)))
        steps.append(pairs)
    return steps


def butterfly_sum(x, axes):
    patch_count, map_count = (lax.axis_size(a) for a in axes)
    if (patch_count, map_count) == (16, 32):
        for pairs in torus_steps(patch_count, map_count):
            x = x + lax.ppermute(x, axes, pairs)
        return x
    for axis in axes:
        count = lax.axis_size(axis)
        step = 1
        while step < count:
            x = x + lax.ppermute(x, axis, [(i, i ^ step) for i in range(count)])
            step *= 2
    return x


def window_kernel(total_blocks, cols_ref, cot_ref, f_ref, tiles_ref, win_ref):
    nb = tiles_ref.shape[0]
    bs = tiles_ref.shape[2]
    win_ref[...] = jnp.zeros(win_ref.shape, win_ref.dtype)
    f = f_ref[2]
    for r in range(nb):
        rows = [
            jnp.dot(f, cot_ref[m, :, r * bs : (r + 1) * bs], preferred_element_type=jnp.float32)
            for m in range(cot_ref.shape[0])
        ]
        g = jnp.concatenate(rows, axis=0).astype(jnp.bfloat16)
        win_ref[r + 2] += jnp.dot(g, tiles_ref[r, 0], preferred_element_type=jnp.float32)
        row = lax.axis_index("patch") * nb + r
        back = row - cols_ref[1, r]
        back = jnp.where(back < 0, back + total_blocks, back)
        ahead = cols_ref[2, r] - row
        ahead = jnp.where(ahead < 0, ahead + total_blocks, ahead)
        back_one = (back == 1).astype(jnp.int32)
        next_one = (ahead == 1).astype(jnp.int32)
        win_ref[r + back_one] += jnp.dot(g, tiles_ref[r, 1], preferred_element_type=jnp.float32)
        win_ref[r + 4 - next_one] += jnp.dot(g, tiles_ref[r, 2], preferred_element_type=jnp.float32)

def first_window(columns, cot, f2, tiles):
    nb, bs = tiles.shape[0], tiles.shape[2]
    rows = cot.shape[0] * f2.shape[1]
    total_blocks = nb * lax.axis_size("patch")
    return pl.pallas_call(
        functools.partial(window_kernel, total_blocks),
        out_shape=jax.ShapeDtypeStruct((nb + 4, rows, bs), jnp.float32),
        in_specs=[pl.BlockSpec(memory_space=pltpu.SMEM)] + [pl.BlockSpec(memory_space=pltpu.VMEM)] * 3,
        out_specs=pl.BlockSpec(memory_space=pltpu.VMEM),
    )(columns, cot, f2, tiles)


def per_device(maps, cotangent, tiles, columns, filters):
    map_count, chan_count, pix_count = maps.shape
    block_count = tiles.shape[0]
    block_size = tiles.shape[2]
    row_count = map_count * chan_count
    patch_count = lax.axis_size("patch")
    total_blocks = block_count * patch_count
    first_block = lax.axis_index("patch") * block_count
    row_ids = first_block + jnp.arange(block_count, dtype=jnp.int32)
    back_one = ((row_ids - columns[:, 1]) % total_blocks == 1)[:, None, None]
    next_one = ((columns[:, 2] - row_ids) % total_blocks == 1)[:, None, None]
    nb = block_count
    to_right = [(i, (i + 1) % patch_count) for i in range(patch_count)]
    to_left = [((i + 1) % patch_count, i) for i in range(patch_count)]

    def exchange(edge_left, edge_right):
        edge_left, edge_right = lax.optimization_barrier((edge_left, edge_right))
        from_right = lax.ppermute(edge_left, "patch", to_left)
        from_left = lax.ppermute(edge_right, "patch", to_right)
        return from_left, from_right

    def to_blocks(field):
        return field.reshape(row_count, nb, block_size).transpose(1, 0, 2)

    def from_blocks(field):
        return field.transpose(1, 0, 2).reshape(map_count, chan_count, pix_count)

    def forward_local(ext):
        s0 = ext[2 : 2 + nb]
        s1 = jnp.where(back_one, ext[1 : 1 + nb], ext[0:nb])
        s2 = jnp.where(next_one, ext[3 : 3 + nb], ext[4 : 4 + nb])
        picked = jnp.stack([s0, s1, s2], axis=1).astype(jnp.bfloat16)
        return jnp.einsum("rjnq,rjiq->rni", picked, tiles, preferred_element_type=jnp.float32)

    def adjoint_window(grads):
        contrib = jnp.einsum("rni,rjiq->rjnq", grads, tiles, preferred_element_type=jnp.float32)
        c0, c1, c2 = contrib[:, 0], contrib[:, 1], contrib[:, 2]
        zero = jnp.zeros_like(c0)
        pad = lambda v, lo: jnp.pad(v, ((lo, 4 - lo), (0, 0), (0, 0)))
        return (
            pad(c0, 2)
            + pad(jnp.where(back_one, c1, zero), 1)
            + pad(jnp.where(back_one, zero, c1), 0)
            + pad(jnp.where(next_one, c2, zero), 3)
            + pad(jnp.where(next_one, zero, c2), 4)
        )

    x_zero = to_blocks(maps)
    cot_b = to_blocks(cotangent).reshape(nb, map_count, chan_count, block_size)
    grads = jnp.einsum("kco,rmop->krmcp", filters, cot_b, preferred_element_type=jnp.float32)
    grads = grads.reshape(3, nb, row_count, block_size)
    grad_two = grads[2].astype(jnp.bfloat16)

    win1 = first_window(columns.T, cotangent, filters, tiles)
    x0f = x_zero.astype(jnp.float32)
    send_left = jnp.stack([x0f[0:2], win1[0:2]])
    send_right = jnp.stack([x0f[nb - 2 : nb], win1[nb + 2 : nb + 4]])
    got_left, got_right = exchange(send_left, send_right)
    ext0 = jnp.concatenate([got_left[0], x0f, got_right[0]], axis=0)
    x_one = forward_local(ext0).astype(jnp.bfloat16)
    adj1 = win1[2 : 2 + nb]
    adj1 = adj1.at[0:2].add(got_left[1])
    adj1 = adj1.at[nb - 2 : nb].add(got_right[1])
    update = (grads[1] + 2.0 * adj1).astype(jnp.bfloat16)

    win2 = adjoint_window(update)
    x1f = x_one.astype(jnp.float32)
    send_left = jnp.stack([x1f[0:2], win2[0:2]])
    send_right = jnp.stack([x1f[nb - 2 : nb], win2[nb + 2 : nb + 4]])
    got_left, got_right = exchange(send_left, send_right)
    ext1 = jnp.concatenate([got_left[0], x1f, got_right[0]], axis=0)
    x_two = (2.0 * forward_local(ext1) - x0f).astype(jnp.bfloat16)
    adj2 = win2[2 : 2 + nb]
    adj2 = adj2.at[0:2].add(got_left[1])
    adj2 = adj2.at[nb - 2 : nb].add(got_right[1])
    input_grad = (grads[0] - grad_two.astype(jnp.float32) + adj2).astype(jnp.bfloat16)

    split = (nb, map_count, chan_count, block_size)
    terms = jnp.stack([x_zero.reshape(split), x_one.reshape(split), x_two.reshape(split)])
    out_b = jnp.einsum("kco,krmcp->rmop", filters, terms, preferred_element_type=jnp.float32)
    output = from_blocks(out_b.astype(jnp.bfloat16).reshape(nb, row_count, block_size))
    scale = 1.0 / math.sqrt(map_count * lax.axis_size("map") * pix_count * patch_count)
    early = jnp.einsum("krmcp,rmop->kco", terms[:2], cot_b, preferred_element_type=jnp.float32)
    late = jnp.einsum("rmcp,rmop->co", terms[2], cot_b, preferred_element_type=jnp.float32)
    local_grad = jnp.concatenate([early, late[None]])
    filter_grad = butterfly_sum(local_grad, ("patch", "map")) * scale
    return (output, from_blocks(input_grad), filter_grad)


def solution(mesh):
    placed = (
        P("map", None, "patch"),
        P("map", None, "patch"),
        P("patch", None, None, None),
        P("patch", None),
        P(),
    )
    return jax.shard_map(
        per_device,
        mesh=mesh,
        in_specs=placed,
        out_specs=(P("map", None, "patch"), P("map", None, "patch"), P()),
        check_vma=False,
    )
```

```python
import math

import jax
import jax.numpy as jnp
from jax import lax
from jax.experimental import pallas as pl
from jax.experimental.pallas import tpu as pltpu
from jax.sharding import PartitionSpec as P

REACH = 2


def ring_partner(coord, size, level):
    if size == 4 and level == 1:
        return (coord + 1) % size if coord % 2 else (coord - 1) % size
    return coord ^ (1 << level)


def torus_steps(patch_count, map_count):
    def coords(p, m):
        return dict(y=p // 4, x=((p // 2) % 2) * 2 + m // 16, z=m % 16, core=p % 2)

    def linear(c):
        p = c["y"] * 4 + (c["x"] // 2) * 2 + c["core"]
        return p * map_count + (c["x"] % 2) * 16 + c["z"]

    sizes = dict(core=2, x=4, y=4, z=16)
    plan = [("core", 0), ("x", 0), ("x", 1), ("y", 0), ("y", 1), ("z", 0), ("z", 1)]
    steps = []
    for name, level in plan:
        pairs = []
        for p in range(patch_count):
            for m in range(map_count):
                c = coords(p, m)
                d = dict(c)
                d[name] = ring_partner(c[name], sizes[name], level)
                pairs.append((linear(c), linear(d)))
        steps.append(pairs)
    for odd_up in (False, True):
        pairs = []
        for p in range(patch_count):
            for m in range(map_count):
                c = coords(p, m)
                d = dict(c)
                g = c["z"] // 4
                if not odd_up:
                    d["z"] = c["z"] ^ 4
                else:
                    d["z"] = (c["z"] + 4) % 16 if g % 2 else (c["z"] - 4) % 16
                pairs.append((linear(c), linear(d)))
        steps.append(pairs)
    return steps


def butterfly_sum(x, axes):
    patch_count, map_count = (lax.axis_size(a) for a in axes)
    if (patch_count, map_count) == (16, 32):
        for pairs in torus_steps(patch_count, map_count):
            x = x + lax.ppermute(x, axes, pairs)
        return x
    for axis in axes:
        count = lax.axis_size(axis)
        step = 1
        while step < count:
            x = x + lax.ppermute(x, axis, [(i, i ^ step) for i in range(count)])
            step *= 2
    return x


def window_kernel(flags_ref, cot_ref, f_ref, tiles_hbm, win_ref, tiles_vmem, sems):
    nb = tiles_vmem.shape[0]
    bs = tiles_vmem.shape[2]
    copies = [pltpu.make_async_copy(tiles_hbm.at[r], tiles_vmem.at[r], sems.at[r]) for r in range(nb)]
    for copy in copies:
        copy.start()
    win_ref[...] = jnp.zeros(win_ref.shape, win_ref.dtype)
    f = f_ref[2]
    for r in range(nb):
        rows = [
            jnp.dot(f, cot_ref[m, :, r * bs : (r + 1) * bs], preferred_element_type=jnp.float32)
            for m in range(cot_ref.shape[0])
        ]
        g = jnp.concatenate(rows, axis=0).astype(jnp.bfloat16)
        copies[r].wait()
        win_ref[r + 2] += jnp.dot(g, tiles_vmem[r, 0], preferred_element_type=jnp.float32)
        win_ref[r + flags_ref[r, 0]] += jnp.dot(g, tiles_vmem[r, 1], preferred_element_type=jnp.float32)
        win_ref[r + 4 - flags_ref[r, 1]] += jnp.dot(g, tiles_vmem[r, 2], preferred_element_type=jnp.float32)


def first_window(flags, cot, f2, tiles):
    nb, bs = tiles.shape[0], tiles.shape[2]
    rows = cot.shape[0] * f2.shape[1]
    vmem = pl.BlockSpec(memory_space=pltpu.VMEM)
    return pl.pallas_call(
        window_kernel,
        out_shape=jax.ShapeDtypeStruct((nb + 4, rows, bs), jnp.float32),
        in_specs=[pl.BlockSpec(memory_space=pltpu.SMEM), vmem, vmem, pl.BlockSpec(memory_space=pl.ANY)],
        out_specs=vmem,
        scratch_shapes=[pltpu.VMEM(tiles.shape, tiles.dtype), pltpu.SemaphoreType.DMA((nb,))],
    )(flags, cot, f2, tiles)


def per_device(maps, cotangent, tiles, columns, filters):
    map_count, chan_count, pix_count = maps.shape
    block_count = tiles.shape[0]
    block_size = tiles.shape[2]
    row_count = map_count * chan_count
    patch_count = lax.axis_size("patch")
    total_blocks = block_count * patch_count
    first_block = lax.axis_index("patch") * block_count
    row_ids = first_block + jnp.arange(block_count, dtype=jnp.int32)
    back_one = ((row_ids - columns[:, 1]) % total_blocks == 1)[:, None, None]
    next_one = ((columns[:, 2] - row_ids) % total_blocks == 1)[:, None, None]
    nb = block_count
    to_right = [(i, (i + 1) % patch_count) for i in range(patch_count)]
    to_left = [((i + 1) % patch_count, i) for i in range(patch_count)]

    def exchange(edge_left, edge_right):
        edge_left, edge_right = lax.optimization_barrier((edge_left, edge_right))
        from_right = lax.ppermute(edge_left, "patch", to_left)
        from_left = lax.ppermute(edge_right, "patch", to_right)
        return from_left, from_right

    def to_blocks(field):
        return field.reshape(row_count, nb, block_size).transpose(1, 0, 2)

    def from_blocks(field):
        return field.transpose(1, 0, 2).reshape(map_count, chan_count, pix_count)

    def forward_local(ext):
        s0 = ext[2 : 2 + nb]
        s1 = jnp.where(back_one, ext[1 : 1 + nb], ext[0:nb])
        s2 = jnp.where(next_one, ext[3 : 3 + nb], ext[4 : 4 + nb])
        picked = jnp.stack([s0, s1, s2], axis=1).astype(jnp.bfloat16)
        return jnp.einsum("rjnq,rjiq->rni", picked, tiles, preferred_element_type=jnp.float32)

    def adjoint_window(grads):
        contrib = jnp.einsum("rni,rjiq->rjnq", grads, tiles, preferred_element_type=jnp.float32)
        c0, c1, c2 = contrib[:, 0], contrib[:, 1], contrib[:, 2]
        zero = jnp.zeros_like(c0)
        pad = lambda v, lo: jnp.pad(v, ((lo, 4 - lo), (0, 0), (0, 0)))
        return (
            pad(c0, 2)
            + pad(jnp.where(back_one, c1, zero), 1)
            + pad(jnp.where(back_one, zero, c1), 0)
            + pad(jnp.where(next_one, c2, zero), 3)
            + pad(jnp.where(next_one, zero, c2), 4)
        )

    x_zero = to_blocks(maps)
    cot_b = to_blocks(cotangent).reshape(nb, map_count, chan_count, block_size)
    grads = jnp.einsum("kco,rmop->krmcp", filters, cot_b, preferred_element_type=jnp.float32)
    grads = grads.reshape(3, nb, row_count, block_size)
    grad_two = grads[2].astype(jnp.bfloat16)

    flags = jnp.stack([back_one[:, 0, 0], next_one[:, 0, 0]], axis=1).astype(jnp.int32)
    win1 = first_window(flags, cotangent, filters, tiles)
    x0f = x_zero.astype(jnp.float32)
    send_left = jnp.stack([x0f[0:2], win1[0:2]])
    send_right = jnp.stack([x0f[nb - 2 : nb], win1[nb + 2 : nb + 4]])
    got_left, got_right = exchange(send_left, send_right)
    ext0 = jnp.concatenate([got_left[0], x0f, got_right[0]], axis=0)
    x_one = forward_local(ext0).astype(jnp.bfloat16)
    adj1 = win1[2 : 2 + nb]
    adj1 = adj1.at[0:2].add(got_left[1])
    adj1 = adj1.at[nb - 2 : nb].add(got_right[1])
    update = (grads[1] + 2.0 * adj1).astype(jnp.bfloat16)

    win2 = adjoint_window(update)
    x1f = x_one.astype(jnp.float32)
    send_left = jnp.stack([x1f[0:2], win2[0:2]])
    send_right = jnp.stack([x1f[nb - 2 : nb], win2[nb + 2 : nb + 4]])
    got_left, got_right = exchange(send_left, send_right)
    ext1 = jnp.concatenate([got_left[0], x1f, got_right[0]], axis=0)
    x_two = (2.0 * forward_local(ext1) - x0f).astype(jnp.bfloat16)
    adj2 = win2[2 : 2 + nb]
    adj2 = adj2.at[0:2].add(got_left[1])
    adj2 = adj2.at[nb - 2 : nb].add(got_right[1])
    input_grad = (grads[0] - grad_two.astype(jnp.float32) + adj2).astype(jnp.bfloat16)

    split = (nb, map_count, chan_count, block_size)
    terms = jnp.stack([x_zero.reshape(split), x_one.reshape(split), x_two.reshape(split)])
    out_b = jnp.einsum("kco,krmcp->rmop", filters, terms, preferred_element_type=jnp.float32)
    output = from_blocks(out_b.astype(jnp.bfloat16).reshape(nb, row_count, block_size))
    scale = 1.0 / math.sqrt(map_count * lax.axis_size("map") * pix_count * patch_count)
    early = jnp.einsum("krmcp,rmop->kco", terms[:2], cot_b, preferred_element_type=jnp.float32)
    late = jnp.einsum("rmcp,rmop->co", terms[2], cot_b, preferred_element_type=jnp.float32)
    local_grad = jnp.concatenate([early, late[None]])
    filter_grad = butterfly_sum(local_grad, ("patch", "map")) * scale
    return (output, from_blocks(input_grad), filter_grad)


def solution(mesh):
    placed = (
        P("map", None, "patch"),
        P("map", None, "patch"),
        P("patch", None, None, None),
        P("patch", None),
        P(),
    )
    return jax.shard_map(
        per_device,
        mesh=mesh,
        in_specs=placed,
        out_specs=(P("map", None, "patch"), P("map", None, "patch"), P()),
        check_vma=False,
    )
```

```python
import math

import jax
import jax.numpy as jnp
from jax import lax
from jax.experimental import pallas as pl
from jax.experimental.pallas import tpu as pltpu
from jax.sharding import PartitionSpec as P

REACH = 2


def ring_partner(coord, size, level):
    if size == 4 and level == 1:
        return (coord + 1) % size if coord % 2 else (coord - 1) % size
    return coord ^ (1 << level)


def torus_steps(patch_count, map_count):
    def coords(p, m):
        return dict(y=p // 4, x=((p // 2) % 2) * 2 + m // 16, z=m % 16, core=p % 2)

    def linear(c):
        p = c["y"] * 4 + (c["x"] // 2) * 2 + c["core"]
        return p * map_count + (c["x"] % 2) * 16 + c["z"]

    sizes = dict(core=2, x=4, y=4, z=16)
    plan = [("core", 0), ("x", 0), ("x", 1), ("y", 0), ("y", 1), ("z", 0), ("z", 1)]
    steps = []
    for name, level in plan:
        pairs = []
        for p in range(patch_count):
            for m in range(map_count):
                c = coords(p, m)
                d = dict(c)
                d[name] = ring_partner(c[name], sizes[name], level)
                pairs.append((linear(c), linear(d)))
        steps.append(pairs)
    for odd_up in (False, True):
        pairs = []
        for p in range(patch_count):
            for m in range(map_count):
                c = coords(p, m)
                d = dict(c)
                g = c["z"] // 4
                if not odd_up:
                    d["z"] = c["z"] ^ 4
                else:
                    d["z"] = (c["z"] + 4) % 16 if g % 2 else (c["z"] - 4) % 16
                pairs.append((linear(c), linear(d)))
        steps.append(pairs)
    return steps[-2:] + steps[:-2]


def butterfly_sum(x, axes):
    patch_count, map_count = (lax.axis_size(a) for a in axes)
    if (patch_count, map_count) == (16, 32):
        for pairs in torus_steps(patch_count, map_count):
            x = x + lax.ppermute(x, axes, pairs)
        return x
    for axis in axes:
        count = lax.axis_size(axis)
        step = 1
        while step < count:
            x = x + lax.ppermute(x, axis, [(i, i ^ step) for i in range(count)])
            step *= 2
    return x


def window_kernel(flags_ref, cot_ref, f_ref, tiles_ref, win_ref):
    nb = tiles_ref.shape[0]
    bs = tiles_ref.shape[2]
    win_ref[...] = jnp.zeros(win_ref.shape, win_ref.dtype)
    f = f_ref[2]
    for r in range(nb):
        rows = [
            jnp.dot(f, cot_ref[m, :, r * bs : (r + 1) * bs], preferred_element_type=jnp.float32)
            for m in range(cot_ref.shape[0])
        ]
        g = jnp.concatenate(rows, axis=0).astype(jnp.bfloat16)
        win_ref[r + 2] += jnp.dot(g, tiles_ref[r, 0], preferred_element_type=jnp.float32)
        win_ref[r + flags_ref[r, 0]] += jnp.dot(g, tiles_ref[r, 1], preferred_element_type=jnp.float32)
        win_ref[r + 4 - flags_ref[r, 1]] += jnp.dot(g, tiles_ref[r, 2], preferred_element_type=jnp.float32)

def first_window(flags, cot, f2, tiles):
    nb, bs = tiles.shape[0], tiles.shape[2]
    rows = cot.shape[0] * f2.shape[1]
    return pl.pallas_call(
        window_kernel,
        out_shape=jax.ShapeDtypeStruct((nb + 4, rows, bs), jnp.float32),
        in_specs=[pl.BlockSpec(memory_space=pltpu.SMEM)] + [pl.BlockSpec(memory_space=pltpu.VMEM)] * 3,
        out_specs=pl.BlockSpec(memory_space=pltpu.VMEM),
    )(flags, cot, f2, tiles)


def per_device(maps, cotangent, tiles, columns, filters):
    map_count, chan_count, pix_count = maps.shape
    block_count = tiles.shape[0]
    block_size = tiles.shape[2]
    row_count = map_count * chan_count
    patch_count = lax.axis_size("patch")
    total_blocks = block_count * patch_count
    first_block = lax.axis_index("patch") * block_count
    row_ids = first_block + jnp.arange(block_count, dtype=jnp.int32)
    back_one = ((row_ids - columns[:, 1]) % total_blocks == 1)[:, None, None]
    next_one = ((columns[:, 2] - row_ids) % total_blocks == 1)[:, None, None]
    nb = block_count
    to_right = [(i, (i + 1) % patch_count) for i in range(patch_count)]
    to_left = [((i + 1) % patch_count, i) for i in range(patch_count)]

    def exchange(edge_left, edge_right):
        edge_left, edge_right = lax.optimization_barrier((edge_left, edge_right))
        from_right = lax.ppermute(edge_left, "patch", to_left)
        from_left = lax.ppermute(edge_right, "patch", to_right)
        return from_left, from_right

    def to_blocks(field):
        return field.reshape(row_count, nb, block_size).transpose(1, 0, 2)

    def from_blocks(field):
        return field.transpose(1, 0, 2).reshape(map_count, chan_count, pix_count)

    def forward_local(ext):
        s0 = ext[2 : 2 + nb]
        s1 = jnp.where(back_one, ext[1 : 1 + nb], ext[0:nb])
        s2 = jnp.where(next_one, ext[3 : 3 + nb], ext[4 : 4 + nb])
        picked = jnp.stack([s0, s1, s2], axis=1).astype(jnp.bfloat16)
        return jnp.einsum("rjnq,rjiq->rni", picked, tiles, preferred_element_type=jnp.float32)

    def adjoint_window(grads):
        contrib = jnp.einsum("rni,rjiq->rjnq", grads, tiles, preferred_element_type=jnp.float32)
        c0, c1, c2 = contrib[:, 0], contrib[:, 1], contrib[:, 2]
        zero = jnp.zeros_like(c0)
        pad = lambda v, lo: jnp.pad(v, ((lo, 4 - lo), (0, 0), (0, 0)))
        return (
            pad(c0, 2)
            + pad(jnp.where(back_one, c1, zero), 1)
            + pad(jnp.where(back_one, zero, c1), 0)
            + pad(jnp.where(next_one, c2, zero), 3)
            + pad(jnp.where(next_one, zero, c2), 4)
        )

    x_zero = to_blocks(maps)
    cot_b = to_blocks(cotangent).reshape(nb, map_count, chan_count, block_size)
    grads = jnp.einsum("kco,rmop->krmcp", filters, cot_b, preferred_element_type=jnp.float32)
    grads = grads.reshape(3, nb, row_count, block_size)
    grad_two = grads[2].astype(jnp.bfloat16)

    flags = jnp.stack([back_one[:, 0, 0], next_one[:, 0, 0]], axis=1).astype(jnp.int32)
    win1 = first_window(flags, cotangent, filters, tiles)
    x0f = x_zero.astype(jnp.float32)
    send_left = jnp.stack([x0f[0:2], win1[0:2]])
    send_right = jnp.stack([x0f[nb - 2 : nb], win1[nb + 2 : nb + 4]])
    got_left, got_right = exchange(send_left, send_right)
    ext0 = jnp.concatenate([got_left[0], x0f, got_right[0]], axis=0)
    x_one = forward_local(ext0).astype(jnp.bfloat16)
    adj1 = win1[2 : 2 + nb]
    adj1 = adj1.at[0:2].add(got_left[1])
    adj1 = adj1.at[nb - 2 : nb].add(got_right[1])
    update = (grads[1] + 2.0 * adj1).astype(jnp.bfloat16)

    win2 = adjoint_window(update)
    x1f = x_one.astype(jnp.float32)
    send_left = jnp.stack([x1f[0:2], win2[0:2]])
    send_right = jnp.stack([x1f[nb - 2 : nb], win2[nb + 2 : nb + 4]])
    got_left, got_right = exchange(send_left, send_right)
    ext1 = jnp.concatenate([got_left[0], x1f, got_right[0]], axis=0)
    x_two = (2.0 * forward_local(ext1) - x0f).astype(jnp.bfloat16)
    adj2 = win2[2 : 2 + nb]
    adj2 = adj2.at[0:2].add(got_left[1])
    adj2 = adj2.at[nb - 2 : nb].add(got_right[1])
    input_grad = (grads[0] - grad_two.astype(jnp.float32) + adj2).astype(jnp.bfloat16)

    split = (nb, map_count, chan_count, block_size)
    terms = jnp.stack([x_zero.reshape(split), x_one.reshape(split), x_two.reshape(split)])
    out_b = jnp.einsum("kco,krmcp->rmop", filters, terms, preferred_element_type=jnp.float32)
    output = from_blocks(out_b.astype(jnp.bfloat16).reshape(nb, row_count, block_size))
    scale = 1.0 / math.sqrt(map_count * lax.axis_size("map") * pix_count * patch_count)
    early = jnp.einsum("krmcp,rmop->kco", terms[:2], cot_b, preferred_element_type=jnp.float32)
    late = jnp.einsum("rmcp,rmop->co", terms[2], cot_b, preferred_element_type=jnp.float32)
    local_grad = jnp.concatenate([early, late[None]])
    filter_grad = butterfly_sum(local_grad, ("patch", "map")) * scale
    return (output, from_blocks(input_grad), filter_grad)


def solution(mesh):
    placed = (
        P("map", None, "patch"),
        P("map", None, "patch"),
        P("patch", None, None, None),
        P("patch", None),
        P(),
    )
    return jax.shard_map(
        per_device,
        mesh=mesh,
        in_specs=placed,
        out_specs=(P("map", None, "patch"), P("map", None, "patch"), P()),
        check_vma=False,
    )
```

```python
import math

import jax
import jax.numpy as jnp
from jax import lax
from jax.experimental import pallas as pl
from jax.experimental.pallas import tpu as pltpu
from jax.sharding import PartitionSpec as P

REACH = 2


def ring_partner(coord, size, level):
    if size == 4 and level == 1:
        return (coord + 1) % size if coord % 2 else (coord - 1) % size
    return coord ^ (1 << level)


def torus_steps(patch_count, map_count):
    def coords(p, m):
        return dict(y=p // 4, x=((p // 2) % 2) * 2 + m // 16, z=m % 16, core=p % 2)

    def linear(c):
        p = c["y"] * 4 + (c["x"] // 2) * 2 + c["core"]
        return p * map_count + (c["x"] % 2) * 16 + c["z"]

    sizes = dict(core=2, x=4, y=4, z=16)
    plan = [("core", 0), ("x", 0), ("x", 1), ("y", 0), ("y", 1), ("z", 0), ("z", 1)]
    steps = []
    for name, level in plan:
        pairs = []
        for p in range(patch_count):
            for m in range(map_count):
                c = coords(p, m)
                d = dict(c)
                d[name] = ring_partner(c[name], sizes[name], level)
                pairs.append((linear(c), linear(d)))
        steps.append(pairs)
    for odd_up in (False, True):
        pairs = []
        for p in range(patch_count):
            for m in range(map_count):
                c = coords(p, m)
                d = dict(c)
                g = c["z"] // 4
                if not odd_up:
                    d["z"] = c["z"] ^ 4
                else:
                    d["z"] = (c["z"] + 4) % 16 if g % 2 else (c["z"] - 4) % 16
                pairs.append((linear(c), linear(d)))
        steps.append(pairs)
    return [steps[i] for i in (7, 8, 6, 2, 4, 1, 3, 5, 0)]


def butterfly_sum(x, axes):
    patch_count, map_count = (lax.axis_size(a) for a in axes)
    if (patch_count, map_count) == (16, 32):
        for pairs in torus_steps(patch_count, map_count):
            x = x + lax.ppermute(x, axes, pairs)
        return x
    for axis in axes:
        count = lax.axis_size(axis)
        step = 1
        while step < count:
            x = x + lax.ppermute(x, axis, [(i, i ^ step) for i in range(count)])
            step *= 2
    return x


def window_kernel(flags_ref, cot_ref, f_ref, tiles_ref, win_ref):
    nb = tiles_ref.shape[0]
    bs = tiles_ref.shape[2]
    win_ref[...] = jnp.zeros(win_ref.shape, win_ref.dtype)
    f = f_ref[2]
    for r in range(nb):
        rows = [
            jnp.dot(f, cot_ref[m, :, r * bs : (r + 1) * bs], preferred_element_type=jnp.float32)
            for m in range(cot_ref.shape[0])
        ]
        g = jnp.concatenate(rows, axis=0).astype(jnp.bfloat16)
        win_ref[r + 2] += jnp.dot(g, tiles_ref[r, 0], preferred_element_type=jnp.float32)
        win_ref[r + flags_ref[r, 0]] += jnp.dot(g, tiles_ref[r, 1], preferred_element_type=jnp.float32)
        win_ref[r + 4 - flags_ref[r, 1]] += jnp.dot(g, tiles_ref[r, 2], preferred_element_type=jnp.float32)

def first_window(flags, cot, f2, tiles):
    nb, bs = tiles.shape[0], tiles.shape[2]
    rows = cot.shape[0] * f2.shape[1]
    return pl.pallas_call(
        window_kernel,
        out_shape=jax.ShapeDtypeStruct((nb + 4, rows, bs), jnp.float32),
        in_specs=[pl.BlockSpec(memory_space=pltpu.SMEM)] + [pl.BlockSpec(memory_space=pltpu.VMEM)] * 3,
        out_specs=pl.BlockSpec(memory_space=pltpu.VMEM),
    )(flags, cot, f2, tiles)


def per_device(maps, cotangent, tiles, columns, filters):
    map_count, chan_count, pix_count = maps.shape
    block_count = tiles.shape[0]
    block_size = tiles.shape[2]
    row_count = map_count * chan_count
    patch_count = lax.axis_size("patch")
    total_blocks = block_count * patch_count
    first_block = lax.axis_index("patch") * block_count
    row_ids = first_block + jnp.arange(block_count, dtype=jnp.int32)
    back_one = ((row_ids - columns[:, 1]) % total_blocks == 1)[:, None, None]
    next_one = ((columns[:, 2] - row_ids) % total_blocks == 1)[:, None, None]
    nb = block_count
    to_right = [(i, (i + 1) % patch_count) for i in range(patch_count)]
    to_left = [((i + 1) % patch_count, i) for i in range(patch_count)]

    def exchange(edge_left, edge_right):
        edge_left, edge_right = lax.optimization_barrier((edge_left, edge_right))
        from_right = lax.ppermute(edge_left, "patch", to_left)
        from_left = lax.ppermute(edge_right, "patch", to_right)
        return from_left, from_right

    def to_blocks(field):
        return field.reshape(row_count, nb, block_size).transpose(1, 0, 2)

    def from_blocks(field):
        return field.transpose(1, 0, 2).reshape(map_count, chan_count, pix_count)

    def forward_local(ext):
        s0 = ext[2 : 2 + nb]
        s1 = jnp.where(back_one, ext[1 : 1 + nb], ext[0:nb])
        s2 = jnp.where(next_one, ext[3 : 3 + nb], ext[4 : 4 + nb])
        picked = jnp.stack([s0, s1, s2], axis=1).astype(jnp.bfloat16)
        return jnp.einsum("rjnq,rjiq->rni", picked, tiles, preferred_element_type=jnp.float32)

    def adjoint_window(grads):
        contrib = jnp.einsum("rni,rjiq->rjnq", grads, tiles, preferred_element_type=jnp.float32)
        c0, c1, c2 = contrib[:, 0], contrib[:, 1], contrib[:, 2]
        zero = jnp.zeros_like(c0)
        pad = lambda v, lo: jnp.pad(v, ((lo, 4 - lo), (0, 0), (0, 0)))
        return (
            pad(c0, 2)
            + pad(jnp.where(back_one, c1, zero), 1)
            + pad(jnp.where(back_one, zero, c1), 0)
            + pad(jnp.where(next_one, c2, zero), 3)
            + pad(jnp.where(next_one, zero, c2), 4)
        )

    x_zero = to_blocks(maps)
    cot_b = to_blocks(cotangent).reshape(nb, map_count, chan_count, block_size)
    grads = jnp.einsum("kco,rmop->krmcp", filters, cot_b, preferred_element_type=jnp.float32)
    grads = grads.reshape(3, nb, row_count, block_size)
    grad_two = grads[2].astype(jnp.bfloat16)

    flags = jnp.stack([back_one[:, 0, 0], next_one[:, 0, 0]], axis=1).astype(jnp.int32)
    win1 = first_window(flags, cotangent, filters, tiles)
    x0f = x_zero.astype(jnp.float32)
    send_left = jnp.stack([x0f[0:2], win1[0:2]])
    send_right = jnp.stack([x0f[nb - 2 : nb], win1[nb + 2 : nb + 4]])
    got_left, got_right = exchange(send_left, send_right)
    ext0 = jnp.concatenate([got_left[0], x0f, got_right[0]], axis=0)
    x_one = forward_local(ext0).astype(jnp.bfloat16)
    adj1 = win1[2 : 2 + nb]
    adj1 = adj1.at[0:2].add(got_left[1])
    adj1 = adj1.at[nb - 2 : nb].add(got_right[1])
    update = (grads[1] + 2.0 * adj1).astype(jnp.bfloat16)

    win2 = adjoint_window(update)
    x1f = x_one.astype(jnp.float32)
    send_left = jnp.stack([x1f[0:2], win2[0:2]])
    send_right = jnp.stack([x1f[nb - 2 : nb], win2[nb + 2 : nb + 4]])
    got_left, got_right = exchange(send_left, send_right)
    ext1 = jnp.concatenate([got_left[0], x1f, got_right[0]], axis=0)
    x_two = (2.0 * forward_local(ext1) - x0f).astype(jnp.bfloat16)
    adj2 = win2[2 : 2 + nb]
    adj2 = adj2.at[0:2].add(got_left[1])
    adj2 = adj2.at[nb - 2 : nb].add(got_right[1])
    input_grad = (grads[0] - grad_two.astype(jnp.float32) + adj2).astype(jnp.bfloat16)

    split = (nb, map_count, chan_count, block_size)
    terms = jnp.stack([x_zero.reshape(split), x_one.reshape(split), x_two.reshape(split)])
    out_b = jnp.einsum("kco,krmcp->rmop", filters, terms, preferred_element_type=jnp.float32)
    output = from_blocks(out_b.astype(jnp.bfloat16).reshape(nb, row_count, block_size))
    scale = 1.0 / math.sqrt(map_count * lax.axis_size("map") * pix_count * patch_count)
    early = jnp.einsum("krmcp,rmop->kco", terms[:2], cot_b, preferred_element_type=jnp.float32)
    late = jnp.einsum("rmcp,rmop->co", terms[2], cot_b, preferred_element_type=jnp.float32)
    local_grad = jnp.concatenate([early, late[None]])
    filter_grad = butterfly_sum(local_grad, ("patch", "map")) * scale
    return (output, from_blocks(input_grad), filter_grad)


def solution(mesh):
    placed = (
        P("map", None, "patch"),
        P("map", None, "patch"),
        P("patch", None, None, None),
        P("patch", None),
        P(),
    )
    return jax.shard_map(
        per_device,
        mesh=mesh,
        in_specs=placed,
        out_specs=(P("map", None, "patch"), P("map", None, "patch"), P()),
        check_vma=False,
    )
```

```python
import math

import jax
import jax.numpy as jnp
from jax import lax
from jax.experimental import pallas as pl
from jax.experimental.pallas import tpu as pltpu
from jax.sharding import PartitionSpec as P

REACH = 2


def ring_partner(coord, size, level):
    if size == 4 and level == 1:
        return (coord + 1) % size if coord % 2 else (coord - 1) % size
    return coord ^ (1 << level)


def torus_steps(patch_count, map_count):
    def coords(p, m):
        return dict(y=p // 4, x=((p // 2) % 2) * 2 + m // 16, z=m % 16, core=p % 2)

    def linear(c):
        p = c["y"] * 4 + (c["x"] // 2) * 2 + c["core"]
        return p * map_count + (c["x"] % 2) * 16 + c["z"]

    sizes = dict(core=2, x=4, y=4, z=16)
    plan = [("core", 0), ("x", 0), ("x", 1), ("y", 0), ("y", 1), ("z", 0), ("z", 1)]
    steps = []
    for name, level in plan:
        pairs = []
        for p in range(patch_count):
            for m in range(map_count):
                c = coords(p, m)
                d = dict(c)
                d[name] = ring_partner(c[name], sizes[name], level)
                pairs.append((linear(c), linear(d)))
        steps.append(pairs)
    for odd_up in (False, True):
        pairs = []
        for p in range(patch_count):
            for m in range(map_count):
                c = coords(p, m)
                d = dict(c)
                g = c["z"] // 4
                if not odd_up:
                    d["z"] = c["z"] ^ 4
                else:
                    d["z"] = (c["z"] + 4) % 16 if g % 2 else (c["z"] - 4) % 16
                pairs.append((linear(c), linear(d)))
        steps.append(pairs)
    return [steps[i] for i in (7, 8, 6, 0, 1, 2, 3, 4, 5)]


def butterfly_sum(x, axes):
    patch_count, map_count = (lax.axis_size(a) for a in axes)
    if (patch_count, map_count) == (16, 32):
        for pairs in torus_steps(patch_count, map_count):
            x = x + lax.ppermute(x, axes, pairs)
        return x
    for axis in axes:
        count = lax.axis_size(axis)
        step = 1
        while step < count:
            x = x + lax.ppermute(x, axis, [(i, i ^ step) for i in range(count)])
            step *= 2
    return x


def window_kernel(flags_ref, cot_ref, f_ref, tiles_ref, win_ref):
    nb = tiles_ref.shape[0]
    bs = tiles_ref.shape[2]
    win_ref[...] = jnp.zeros(win_ref.shape, win_ref.dtype)
    f = f_ref[2]
    for r in range(nb):
        rows = [
            jnp.dot(f, cot_ref[m, :, r * bs : (r + 1) * bs], preferred_element_type=jnp.float32)
            for m in range(cot_ref.shape[0])
        ]
        g = jnp.concatenate(rows, axis=0).astype(jnp.bfloat16)
        win_ref[r + 2] += jnp.dot(g, tiles_ref[r, 0], preferred_element_type=jnp.float32)
        win_ref[r + flags_ref[r, 0]] += jnp.dot(g, tiles_ref[r, 1], preferred_element_type=jnp.float32)
        win_ref[r + 4 - flags_ref[r, 1]] += jnp.dot(g, tiles_ref[r, 2], preferred_element_type=jnp.float32)

def first_window(flags, cot, f2, tiles):
    nb, bs = tiles.shape[0], tiles.shape[2]
    rows = cot.shape[0] * f2.shape[1]
    return pl.pallas_call(
        window_kernel,
        out_shape=jax.ShapeDtypeStruct((nb + 4, rows, bs), jnp.float32),
        in_specs=[pl.BlockSpec(memory_space=pltpu.SMEM)] + [pl.BlockSpec(memory_space=pltpu.VMEM)] * 3,
        out_specs=pl.BlockSpec(memory_space=pltpu.VMEM),
    )(flags, cot, f2, tiles)


def per_device(maps, cotangent, tiles, columns, filters):
    map_count, chan_count, pix_count = maps.shape
    block_count = tiles.shape[0]
    block_size = tiles.shape[2]
    row_count = map_count * chan_count
    patch_count = lax.axis_size("patch")
    total_blocks = block_count * patch_count
    first_block = lax.axis_index("patch") * block_count
    row_ids = first_block + jnp.arange(block_count, dtype=jnp.int32)
    back_one = ((row_ids - columns[:, 1]) % total_blocks == 1)[:, None, None]
    next_one = ((columns[:, 2] - row_ids) % total_blocks == 1)[:, None, None]
    nb = block_count
    to_right = [(i, (i + 1) % patch_count) for i in range(patch_count)]
    to_left = [((i + 1) % patch_count, i) for i in range(patch_count)]

    def exchange(edge_left, edge_right):
        edge_left, edge_right = lax.optimization_barrier((edge_left, edge_right))
        from_right = lax.ppermute(edge_left, "patch", to_left)
        from_left = lax.ppermute(edge_right, "patch", to_right)
        return from_left, from_right

    def to_blocks(field):
        return field.reshape(row_count, nb, block_size).transpose(1, 0, 2)

    def from_blocks(field):
        return field.transpose(1, 0, 2).reshape(map_count, chan_count, pix_count)

    def forward_local(ext):
        s0 = ext[2 : 2 + nb]
        s1 = jnp.where(back_one, ext[1 : 1 + nb], ext[0:nb])
        s2 = jnp.where(next_one, ext[3 : 3 + nb], ext[4 : 4 + nb])
        picked = jnp.stack([s0, s1, s2], axis=1).astype(jnp.bfloat16)
        return jnp.einsum("rjnq,rjiq->rni", picked, tiles, preferred_element_type=jnp.float32)

    def adjoint_window(grads):
        contrib = jnp.einsum("rni,rjiq->rjnq", grads, tiles, preferred_element_type=jnp.float32)
        c0, c1, c2 = contrib[:, 0], contrib[:, 1], contrib[:, 2]
        zero = jnp.zeros_like(c0)
        pad = lambda v, lo: jnp.pad(v, ((lo, 4 - lo), (0, 0), (0, 0)))
        return (
            pad(c0, 2)
            + pad(jnp.where(back_one, c1, zero), 1)
            + pad(jnp.where(back_one, zero, c1), 0)
            + pad(jnp.where(next_one, c2, zero), 3)
            + pad(jnp.where(next_one, zero, c2), 4)
        )

    x_zero = to_blocks(maps)
    cot_b = to_blocks(cotangent).reshape(nb, map_count, chan_count, block_size)
    grads = jnp.einsum("kco,rmop->krmcp", filters, cot_b, preferred_element_type=jnp.float32)
    grads = grads.reshape(3, nb, row_count, block_size)
    grad_two = grads[2].astype(jnp.bfloat16)

    flags = jnp.stack([back_one[:, 0, 0], next_one[:, 0, 0]], axis=1).astype(jnp.int32)
    win1 = first_window(flags, cotangent, filters, tiles)
    x0f = x_zero.astype(jnp.float32)
    send_left = jnp.stack([x0f[0:2], win1[0:2]])
    send_right = jnp.stack([x0f[nb - 2 : nb], win1[nb + 2 : nb + 4]])
    got_left, got_right = exchange(send_left, send_right)
    ext0 = jnp.concatenate([got_left[0], x0f, got_right[0]], axis=0)
    x_one = forward_local(ext0).astype(jnp.bfloat16)
    adj1 = win1[2 : 2 + nb]
    adj1 = adj1.at[0:2].add(got_left[1])
    adj1 = adj1.at[nb - 2 : nb].add(got_right[1])
    update = (grads[1] + 2.0 * adj1).astype(jnp.bfloat16)

    win2 = adjoint_window(update)
    x1f = x_one.astype(jnp.float32)
    send_left = jnp.stack([x1f[0:2], win2[0:2]])
    send_right = jnp.stack([x1f[nb - 2 : nb], win2[nb + 2 : nb + 4]])
    got_left, got_right = exchange(send_left, send_right)
    ext1 = jnp.concatenate([got_left[0], x1f, got_right[0]], axis=0)
    x_two = (2.0 * forward_local(ext1) - x0f).astype(jnp.bfloat16)
    adj2 = win2[2 : 2 + nb]
    adj2 = adj2.at[0:2].add(got_left[1])
    adj2 = adj2.at[nb - 2 : nb].add(got_right[1])
    input_grad = (grads[0] - grad_two.astype(jnp.float32) + adj2).astype(jnp.bfloat16)

    split = (nb, map_count, chan_count, block_size)
    terms = jnp.stack([x_zero.reshape(split), x_one.reshape(split), x_two.reshape(split)])
    out_b = jnp.einsum("kco,krmcp->rmop", filters, terms, preferred_element_type=jnp.float32)
    output = from_blocks(out_b.astype(jnp.bfloat16).reshape(nb, row_count, block_size))
    scale = 1.0 / math.sqrt(map_count * lax.axis_size("map") * pix_count * patch_count)
    early = jnp.einsum("krmcp,rmop->kco", terms[:2], cot_b, preferred_element_type=jnp.float32)
    late = jnp.einsum("rmcp,rmop->co", terms[2], cot_b, preferred_element_type=jnp.float32)
    local_grad = jnp.concatenate([early, late[None]])
    filter_grad = butterfly_sum(local_grad, ("patch", "map")) * scale
    return (output, from_blocks(input_grad), filter_grad)


def solution(mesh):
    placed = (
        P("map", None, "patch"),
        P("map", None, "patch"),
        P("patch", None, None, None),
        P("patch", None),
        P(),
    )
    return jax.shard_map(
        per_device,
        mesh=mesh,
        in_specs=placed,
        out_specs=(P("map", None, "patch"), P("map", None, "patch"), P()),
        check_vma=False,
    )
```
